512 devices in a mesh: section: 2 (over core), dp: 64 (over z, x), mp: 4 (over y).
Axes of the slice: x: 4, y: 4, z: 16, core: 2. Of those that a mesh axis runs over, the one named last changes fastest.
Arguments:
- states: bfloat16 [512, 24, 4096], P('dp')
- norm_gain: float32 [4096], replicated, may hold values from 0.1 to 1.9
- key_weight: bfloat16 [4096, 4096], P('dp', ('section', 'mp')), may hold values from -0.09375 to 0.09375
- value_weight: bfloat16 [4096, 4096], P('dp', ('section', 'mp')), may hold values from -0.09375 to 0.09375
- pass_len: int32 [512], P('dp'), may hold values from 1 to 24
- retrieval: int32 [64, 64], replicated, may hold values from 0 to 511, as said below
- queries: bfloat16 [64, 32, 4096], P('dp', None, ('section', 'mp'))
Outputs:
- context: bfloat16 [64, 32, 4096], P('dp', None, ('section', 'mp'))
- passage_scores: float32 [64, 64], P('dp')
The draws below stay inside these ranges and needn't reach their ends.
Inputs may be any that keep to these rules, and one draw needn't show every extreme that they name: `retrieval`: each question's list names 64 different passages. Counting passages of one block of 8 ids (the same id // 8), a list names passages of between 32 and 63 different blocks, at most 2 from any block, and exactly 2 from at least one. Popular passages recur in many lists.
All inputs are finite; a program needn't handle non-finite values.
Results may differ from the reference program's by a relative error of at most 0.013.
Values may be sent and summed in bfloat16 or wider, within the bound.
No kernel may reach another device: no remote copies, remote signals or barrier semaphores. Data moves between devices by JAX's collectives and lax.ppermute only.
A program may use at most 128 MiB of HBM per device.

```python
import jax
import jax.numpy as jnp
from jax import lax

D = 4096
HEADS = 64
HS = 64
P_DEV = 8
PLEN = 24
QLEN = 32
QUESTIONS = 64
K_RET = 64
PASSAGES = 512


def draw_states(key, part):
    noise_key, row_key, column_key = jax.random.split(key, 3)
    shape_here = (PASSAGES, PLEN, D)
    base = jax.random.normal(noise_key, shape_here, jnp.float32)
    row_scale = jnp.exp(jax.random.uniform(row_key, (PASSAGES, PLEN, 1), jnp.float32, 0.0, 2.3))
    column_scale = jnp.exp(jax.random.uniform(column_key, (1, 1, D), jnp.float32, -0.7, 0.7))
    return (base * row_scale * column_scale).astype(jnp.bfloat16)


def draw_queries(key, part):
    shape_here = (QUESTIONS, QLEN, HEADS * HS)
    base = 0.3 * jax.random.normal(key, shape_here, jnp.float32)
    return base.astype(jnp.bfloat16)


def draw_retrieval(key, part):

    def one_list(list_key):
        perm_key, count_key, first_key, second_key, step_key, shuffle_key = jax.random.split(list_key, 6)
        owner_order = jax.random.permutation(perm_key, K_RET).astype(jnp.int32)
        doubled = jax.random.randint(count_key, (), 1, K_RET // 2 + 1)
        single = K_RET - doubled
        position = jnp.arange(K_RET, dtype=jnp.int32)
        source = jnp.where(position < single, position, position - single)
        first_pick = jnp.minimum(jax.random.randint(first_key, (K_RET,), 0, P_DEV), jax.random.randint(second_key, (K_RET,), 0, P_DEV))
        step_size = jax.random.randint(step_key, (K_RET,), 1, P_DEV)
        local_pick = jnp.where(position < single, first_pick[source], (first_pick[source] + step_size[source]) % P_DEV)
        chosen = owner_order[source] * P_DEV + local_pick
        return chosen[jax.random.permutation(shuffle_key, K_RET)]
    return jax.vmap(one_list)(jax.random.split(key, QUESTIONS)).astype(jnp.int32)


def place_ends(result, own_key, smallest, high):
    longest = result.shape.index(max(result.shape))
    spots = []
    for shift in (0, 1):
        where = [jax.random.randint(jax.random.fold_in(own_key, axis), (), 0, length) for axis, length in enumerate(result.shape)]
        where[longest] = (where[longest] + shift) % result.shape[longest]
        spots.append(tuple(where))
    return result.at[spots[0]].set(smallest).at[spots[1]].set(high)


def block_scale(stream_key, extent, cuts, smallest, top_value):
    def one(dim, shards_of):
        draws = jax.random.uniform(jax.random.fold_in(jax.random.fold_in(stream_key, 6), dim), (shards_of,), jnp.float32, smallest / len(cuts), top_value / len(cuts))
        return jnp.repeat(jnp.exp(draws), extent[dim] // shards_of).reshape((-1,) + (1,) * (len(extent) - dim - 1))

    level = one(*cuts[0])
    for cut in cuts[1:]:
        level = level * one(*cut)
    return level


def normal_values(rng, shape, spread, reach, cuts=(), kind=jnp.bfloat16):
    loudness = block_scale(rng, shape, cuts, -0.22, 0.18) if cuts else 1.0
    array = jax.random.normal(rng, shape, jnp.float32) * spread * loudness
    return jnp.minimum(jnp.maximum(array, -reach), reach).astype(kind)


def setup_inputs(seed: int = 0) -> dict:
    key_list = jax.random.split(jax.random.key(seed), 8)
    return {
        "states": draw_states(jax.random.fold_in(key_list[7], 71), 0),
        "norm_gain": jnp.clip(1.0 + 0.18 * jax.random.normal(key_list[1], (D,), jnp.float32), 0.1, 1.9),
        "key_weight": normal_values(key_list[2], (D, HEADS * HS), D ** -0.5, 0.09375, ((0, 64), (1, 8))),
        "value_weight": normal_values(key_list[3], (D, HEADS * HS), D ** -0.5, 0.09375, ((0, 64), (1, 8))),
        "pass_len": place_ends(jax.random.randint(key_list[4], (PASSAGES,), 1, PLEN + 1), jax.random.fold_in(key_list[4], 1), 1, PLEN).astype(jnp.int32),
        "retrieval": draw_retrieval(jax.random.fold_in(key_list[7], 71), 0),
        "queries": draw_queries(jax.random.fold_in(key_list[7], 71), 0),
    }


def reference(states, norm_gain, key_weight, value_weight, pass_len, retrieval, queries):
    widened = states.astype(jnp.float32)
    mean_square = lax.optimization_barrier(jnp.mean(widened * widened, axis=-1, keepdims=True))
    normed = (widened * lax.rsqrt(mean_square + 1e-06) * norm_gain).astype(jnp.bfloat16)
    flat_rows = normed.reshape(PASSAGES * PLEN, D)
    keys = jnp.dot(flat_rows, key_weight, preferred_element_type=jnp.float32).astype(jnp.bfloat16)
    values = jnp.dot(flat_rows, value_weight, preferred_element_type=jnp.float32).astype(jnp.bfloat16)
    keys = keys.reshape(PASSAGES, PLEN, HEADS, HS)
    values = values.reshape(PASSAGES, PLEN, HEADS, HS)
    offsets = jnp.arange(PLEN, dtype=jnp.int32)

    def per_question(pair):
        passage_ids, question_rows = pair
        passage_ids = passage_ids.astype(jnp.int32)
        chosen_keys = keys[passage_ids].reshape(K_RET * PLEN, HEADS, HS)
        chosen_values = values[passage_ids].reshape(K_RET * PLEN, HEADS, HS)
        is_live = (offsets[None, :] < pass_len[passage_ids][:, None]).reshape(K_RET * PLEN)
        query_heads = question_rows.reshape(QLEN, HEADS, HS)
        scores = jnp.einsum('thd,lhd->htl', query_heads.astype(jnp.float32), chosen_keys.astype(jnp.float32))
        scores = jnp.where(is_live[None, None, :], scores, -jnp.inf)
        row_max = lax.optimization_barrier(jnp.max(scores, axis=-1, keepdims=True))
        exponent = jnp.exp(scores - row_max)
        row_total = lax.optimization_barrier(jnp.sum(exponent, axis=-1, keepdims=True))
        weights = exponent / row_total
        context = jnp.einsum('htl,lhd->thd', weights, chosen_values.astype(jnp.float32), precision=lax.Precision.HIGHEST)
        context = context.reshape(QLEN, HEADS * HS).astype(jnp.bfloat16)
        passage_mass = weights.reshape(HEADS, QLEN, K_RET, PLEN).sum(axis=-1).sum(axis=0).mean(axis=0)
        return (context, passage_mass)
    context, passage_scores = lax.map(per_question, (retrieval, queries))
    return (context, passage_scores)
```

```python
import jax
import jax.numpy as jnp
from jax import lax
from jax.sharding import PartitionSpec as P

HS = 64
WIRE = jnp.bfloat16


def _plane_shape(mesh):
    n_dp = mesh.shape["dp"]
    try:
        xs = {d.coords[0] for d in mesh.devices[0, :, 0]}
        nx = len(xs)
    except Exception:
        nx = 2 if n_dp % 2 == 0 else 1
    return n_dp // nx, nx


def _ring_perm(nz, nx, along, step):
    pairs = []
    for z in range(nz):
        for x in range(nx):
            if along == "x":
                dst = z * nx + (x + step) % nx
            else:
                dst = ((z + step) % nz) * nx + x
            pairs.append((z * nx + x, dst))
    return pairs


def _send(tree, perm):
    return jax.tree.map(lambda a: lax.ppermute(a, "dp", perm), tree)


def _gather_ring(block, n, fwd, bwd):
    if n == 1:
        return block[None]
    rel = [None] * n
    rel[0] = block
    f = block
    g = block
    for k in range(1, (n - 1) // 2 + 1):
        f = lax.ppermute(f, "dp", fwd)
        g = lax.ppermute(g, "dp", bwd)
        rel[n - k] = f
        rel[k] = g
    if n % 2 == 0:
        half = n // 2
        if block.shape[0] >= 2:
            cut = block.shape[0] // 2
            a = lax.ppermute(f[:cut], "dp", fwd)
            b = lax.ppermute(g[cut:], "dp", bwd)
            rel[half] = jnp.concatenate([a, b], axis=0)
        else:
            rel[half] = lax.ppermute(f, "dp", fwd)
    return jnp.stack(rel)


def _combine(a, b):
    ma, la, oa, ea = a
    mb, lb, ob, eb = b
    m = jnp.maximum(ma, mb)
    sa = jnp.where(ma == m, 1.0, jnp.exp(ma - m))
    sb = jnp.where(mb == m, 1.0, jnp.exp(mb - m))
    l = sa * la + sb * lb
    sa_o = jnp.swapaxes(sa, -1, -2)[..., None]
    sb_o = jnp.swapaxes(sb, -1, -2)[..., None]
    o = oa * sa_o + ob * sb_o
    e = ea * sa[..., None] + eb * sb[..., None]
    return (m, l, o, e)


def _to_wire(s):
    m, l, o, e = s
    return (m, l, o.astype(WIRE), e.astype(WIRE))


def _from_wire(s):
    m, l, o, e = s
    return (m, l, o.astype(jnp.float32), e.astype(jnp.float32))


def _reduce_ring(state, axis, me, n, fwd, bwd):
    def chunk(r):
        idx = (me + r) % n
        return jax.tree.map(lambda a: lax.dynamic_index_in_dim(a, idx, axis, keepdims=False), state)

    if n == 1:
        return chunk(0)
    nb = n // 2
    nf = n - 1 - nb
    bacc = chunk(n - nb)
    facc = None
    result = None
    for k in range(1, nb + 1):
        if nf > 0 and k == nb - nf + 1:
            facc = chunk(nf)
        recv_b = _from_wire(_send(_to_wire(bacc), bwd))
        recv_f = _from_wire(_send(_to_wire(facc), fwd)) if facc is not None else None
        if k < nb:
            bacc = _combine(recv_b, chunk((k - nb) % n))
            if recv_f is not None:
                facc = _combine(recv_f, chunk(nb - k))
        else:
            result = _combine(chunk(0), recv_b)
            if recv_f is not None:
                result = _combine(result, recv_f)
    return result


def _local(nz, nx, states, norm_gain, key_weight, value_weight, pass_len, retrieval, queries):
    blocks, tokens, model_width = states.shape
    inner = key_weight.shape[1]
    heads = inner // HS
    rows_here = key_weight.shape[0]
    n_dp = nz * nx
    dpi = lax.axis_index("dp")
    zi = dpi // nx
    xi = dpi % nx
    xf = _ring_perm(nz, nx, "x", 1)
    xb = _ring_perm(nz, nx, "x", -1)
    zf = _ring_perm(nz, nx, "z", 1)
    zb = _ring_perm(nz, nx, "z", -1)

    wkv = jnp.concatenate([key_weight, value_weight], axis=1)
    wx = _gather_ring(wkv, nx, xf, xb)
    wzx = _gather_ring(wx, nz, zf, zb)

    q_all = lax.all_gather(queries, "dp", axis=0, tiled=True)

    widened = states.astype(jnp.float32)
    mean_square = jnp.mean(widened * widened, axis=-1, keepdims=True)
    normed = (widened * lax.rsqrt(mean_square + 1e-06) * norm_gain).astype(jnp.bfloat16)
    flat = normed.reshape(blocks * tokens, nz, nx, rows_here)
    flat = jnp.roll(flat, -zi, axis=1)
    flat = jnp.roll(flat, -xi, axis=2)
    kv = jnp.dot(
        flat.reshape(blocks * tokens, model_width),
        wzx.reshape(model_width, 2 * inner),
        preferred_element_type=jnp.float32,
    ).astype(jnp.bfloat16)
    keys = kv[:, :inner].reshape(blocks, tokens, heads, HS)
    values = kv[:, inner:].reshape(blocks, tokens, heads, HS)

    n_q, answer_len, _ = q_all.shape
    q_heads = q_all.reshape(n_q, answer_len, heads, HS)
    scores = jnp.einsum("qthe,pshe->qhtps", q_heads, keys, preferred_element_type=jnp.float32)
    local_ids = retrieval - dpi * blocks
    owned = (local_ids >= 0) & (local_ids < blocks)
    onehot = (local_ids[:, None, :] == jnp.arange(blocks, dtype=jnp.int32)[None, :, None]) & owned[:, None, :]
    picked = jnp.any(onehot, axis=2)
    positions = jnp.arange(tokens, dtype=jnp.int32)
    live = picked[:, :, None] & (positions[None, None, :] < pass_len[None, :, None])
    live5 = live[:, None, None, :, :]
    masked = jnp.where(live5, scores, -jnp.inf)
    m_loc = jnp.max(masked, axis=(3, 4))
    e = jnp.where(live5, jnp.exp(scores - m_loc[..., None, None]), 0.0)
    l_loc = jnp.sum(e, axis=(3, 4))
    e_pass = jnp.sum(e, axis=4)
    e_slot = jnp.einsum(
        "qhtp,qpj->qhtj", e_pass, onehot.astype(jnp.float32), precision=lax.Precision.HIGHEST
    )
    o_loc = jnp.einsum(
        "qhtps,pshe->qthe", e, values.astype(jnp.float32), precision=lax.Precision.HIGHEST
    )

    n_local_q = n_q // n_dp
    def split_q(a):
        return a.reshape((nz, nx, n_local_q) + a.shape[1:])
    state = jax.tree.map(split_q, (m_loc, l_loc, o_loc, e_slot))
    state = _reduce_ring(state, 1, xi, nx, xf, xb)
    state = _reduce_ring(state, 0, zi, nz, zf, zb)
    m_fin, l_fin, o_fin, e_fin = state
    context = o_fin / jnp.swapaxes(l_fin, -1, -2)[..., None]
    context = context.reshape(n_local_q, answer_len, inner).astype(jnp.bfloat16)
    mass = jnp.sum(e_fin / l_fin[..., None], axis=(1, 2)) / answer_len
    mass = lax.psum(mass, ("section", "mp"))
    return (context, mass)


def solution(mesh):
    nz, nx = _plane_shape(mesh)
    in_specs = (
        P("dp", None, None),
        P(),
        P("dp", ("section", "mp")),
        P("dp", ("section", "mp")),
        P("dp"),
        P(),
        P("dp", None, ("section", "mp")),
    )
    out_specs = (P("dp", None, ("section", "mp")), P("dp", None))

    def body(*args):
        return _local(nz, nx, *args)

    return jax.shard_map(body, mesh=mesh, in_specs=in_specs, out_specs=out_specs, check_vma=False)
```

```python
import jax
import jax.numpy as jnp
from jax import lax
from jax.sharding import PartitionSpec as P

HS = 64
WIRE = jnp.bfloat16


def _plane_shape(mesh):
    n_dp = mesh.shape["dp"]
    try:
        xs = {d.coords[0] for d in mesh.devices[0, :, 0]}
        nx = len(xs)
    except Exception:
        nx = 2 if n_dp % 2 == 0 else 1
    return n_dp // nx, nx


def _ring_perm(nz, nx, along, step):
    pairs = []
    for z in range(nz):
        for x in range(nx):
            if along == "x":
                dst = z * nx + (x + step) % nx
            else:
                dst = ((z + step) % nz) * nx + x
            pairs.append((z * nx + x, dst))
    return pairs


def _gather_ring(block, n, fwd, bwd):
    if n == 1:
        return block[None]
    rel = [None] * n
    rel[0] = block
    f = block
    g = block
    for k in range(1, (n - 1) // 2 + 1):
        f = lax.ppermute(f, "dp", fwd)
        g = lax.ppermute(g, "dp", bwd)
        rel[n - k] = f
        rel[k] = g
    if n % 2 == 0:
        half = n // 2
        if block.shape[0] >= 2:
            cut = block.shape[0] // 2
            a = lax.ppermute(f[:cut], "dp", fwd)
            b = lax.ppermute(g[cut:], "dp", bwd)
            rel[half] = jnp.concatenate([a, b], axis=0)
        else:
            rel[half] = lax.ppermute(f, "dp", fwd)
    return jnp.stack(rel)


def _combine(a, b):
    ma, la, oa, ea = a
    mb, lb, ob, eb = b
    m = jnp.maximum(ma, mb)
    sa = jnp.where(ma == m, 1.0, jnp.exp(ma - m))
    sb = jnp.where(mb == m, 1.0, jnp.exp(mb - m))
    l = sa * la + sb * lb
    sa_o = jnp.swapaxes(sa, -1, -2)[..., None]
    sb_o = jnp.swapaxes(sb, -1, -2)[..., None]
    o = oa * sa_o + ob * sb_o
    e = ea * sa[..., None] + eb * sb[..., None]
    return (m, l, o, e)


def _split_terms(a, terms):
    big = jnp.float32(3.38e38)
    head = lax.reduce_precision(jnp.clip(a, -big, big), exponent_bits=8, mantissa_bits=7)
    head = jnp.where(jnp.isinf(a), a, head)
    out = [head.astype(WIRE)]
    rest = jnp.where(jnp.isinf(a), 0.0, a - head)
    for _ in range(terms - 1):
        t = lax.reduce_precision(rest, exponent_bits=8, mantissa_bits=7)
        out.append(t.astype(WIRE))
        rest = rest - t
    return out


def _to_wire(s):
    m, l, o, e = s
    lead = m.shape[:-2]
    parts = _split_terms(m, 3) + _split_terms(l, 2) + [o.astype(WIRE), e.astype(WIRE)]
    return jnp.concatenate([p.reshape(lead + (-1,)) for p in parts], axis=-1)


def _from_wire(w, shapes):
    m_shape, o_shape, e_shape = shapes
    lead = w.shape[:-1]
    n_m = 1
    for d in m_shape:
        n_m *= d
    n_o = 1
    for d in o_shape:
        n_o *= d
    pieces = []
    at = 0
    for size in (n_m, n_m, n_m, n_m, n_m, n_o):
        pieces.append(w[..., at:at + size].astype(jnp.float32))
        at += size
    pieces.append(w[..., at:].astype(jnp.float32))
    m = (pieces[0] + pieces[1]) + pieces[2]
    l = pieces[3] + pieces[4]
    return (
        m.reshape(lead + m_shape),
        l.reshape(lead + m_shape),
        pieces[5].reshape(lead + o_shape),
        pieces[6].reshape(lead + e_shape),
    )


def _shapes(s):
    m, l, o, e = s
    return (m.shape[-2:], o.shape[-3:], e.shape[-3:])


def _xfer(s, perm):
    return _from_wire(lax.ppermute(_to_wire(s), "dp", perm), _shapes(s))


def _halving(state, me, n, perm_of):
    bit = 1
    while bit < n:
        size = state[0].shape[0]
        mine = (me // bit) % 2
        pairs = jax.tree.map(lambda a: a.reshape((size // 2, 2) + a.shape[1:]), state)
        keep = jax.tree.map(lambda a: lax.dynamic_index_in_dim(a, mine, 1, keepdims=False), pairs)
        give = jax.tree.map(lambda a: lax.dynamic_index_in_dim(a, 1 - mine, 1, keepdims=False), pairs)
        state = _combine(keep, _xfer(give, perm_of(bit)))
        bit *= 2
    return jax.tree.map(lambda a: a[0], state)


def _reduce_ring(state, axis, me, n, fwd, bwd):
    def chunk(r):
        idx = (me + r) % n
        return jax.tree.map(lambda a: lax.dynamic_index_in_dim(a, idx, axis, keepdims=False), state)

    if n == 1:
        return chunk(0)
    nb = n // 2
    nf = n - 1 - nb
    bacc = chunk(n - nb)
    facc = None
    result = None
    for k in range(1, nb + 1):
        if nf > 0 and k == nb - nf + 1:
            facc = chunk(nf)
        recv_b = _xfer(bacc, bwd)
        recv_f = _xfer(facc, fwd) if facc is not None else None
        if k < nb:
            bacc = _combine(recv_b, chunk((k - nb) % n))
            if recv_f is not None:
                facc = _combine(recv_f, chunk(nb - k))
        else:
            result = _combine(chunk(0), recv_b)
            if recv_f is not None:
                result = _combine(result, recv_f)
    return result


def _local(nz, nx, states, norm_gain, key_weight, value_weight, pass_len, retrieval, queries):
    blocks, tokens, model_width = states.shape
    inner = key_weight.shape[1]
    heads = inner // HS
    rows_here = key_weight.shape[0]
    n_dp = nz * nx
    dpi = lax.axis_index("dp")
    zi = dpi // nx
    xi = dpi % nx
    xf = _ring_perm(nz, nx, "x", 1)
    xb = _ring_perm(nz, nx, "x", -1)
    zf = _ring_perm(nz, nx, "z", 1)
    zb = _ring_perm(nz, nx, "z", -1)

    n_lq, answer_len, _ = queries.shape
    q_rows = queries.reshape(-1, 2 * inner)
    wkv = jnp.concatenate([key_weight, value_weight], axis=1)
    wkv = jnp.concatenate([wkv, q_rows], axis=0)
    wx = _gather_ring(wkv, nx, xf, xb)
    wzx = _gather_ring(wx, nz, zf, zb)
    q_rel = wzx[:, :, rows_here:, :].reshape(nz, nx, n_lq, answer_len, inner)
    q_rel = jnp.roll(jnp.roll(q_rel, zi, axis=0), xi, axis=1)
    q_all = q_rel.reshape(n_dp * n_lq, answer_len, inner)
    wzx = wzx[:, :, :rows_here, :]

    widened = states.astype(jnp.float32)
    mean_square = jnp.mean(widened * widened, axis=-1, keepdims=True)
    normed = (widened * lax.rsqrt(mean_square + 1e-06) * norm_gain).astype(jnp.bfloat16)
    flat = normed.reshape(blocks * tokens, nz, nx, rows_here)
    flat = jnp.roll(flat, -zi, axis=1)
    flat = jnp.roll(flat, -xi, axis=2)
    kv = jnp.dot(
        flat.reshape(blocks * tokens, model_width),
        wzx.reshape(model_width, 2 * inner),
        preferred_element_type=jnp.float32,
    ).astype(jnp.bfloat16)
    keys = kv[:, :inner].reshape(blocks, tokens, heads, HS)
    values = kv[:, inner:].reshape(blocks, tokens, heads, HS)

    n_q = q_all.shape[0]
    n_ps = blocks * tokens
    q_h = jnp.swapaxes(q_all.reshape(n_q * answer_len, heads, HS), 0, 1)
    k_h = jnp.swapaxes(keys.reshape(n_ps, heads, HS), 0, 1)
    v_h = jnp.swapaxes(values.reshape(n_ps, heads, HS), 0, 1)
    scores = jnp.einsum("hie,hje->hij", q_h, k_h, preferred_element_type=jnp.float32)
    scores = scores.reshape(heads, n_q, answer_len, n_ps)
    local_ids = retrieval - dpi * blocks
    owned = (local_ids >= 0) & (local_ids < blocks)
    onehot = (local_ids[:, None, :] == jnp.arange(blocks, dtype=jnp.int32)[None, :, None]) & owned[:, None, :]
    picked = jnp.any(onehot, axis=2)
    positions = jnp.arange(tokens, dtype=jnp.int32)
    live = picked[:, :, None] & (positions[None, None, :] < pass_len[None, :, None])
    live4 = live.reshape(1, n_q, 1, n_ps)
    m_loc = jnp.max(jnp.where(live4, scores, -jnp.inf), axis=3)
    e = jnp.where(live4, jnp.exp(scores - m_loc[..., None]), 0.0)
    l_loc = jnp.sum(e, axis=3)
    e_parts = _split_terms(e.reshape(heads, n_q * answer_len, n_ps), 2)
    o_h = sum(
        jnp.einsum("hij,hje->hie", part, v_h, preferred_element_type=jnp.float32) for part in e_parts
    )
    block_of = (jnp.arange(n_ps, dtype=jnp.int32)[:, None] // tokens) == jnp.arange(blocks, dtype=jnp.int32)[None, :]
    e_pass = sum(
        jnp.einsum("hij,jp->hip", part, block_of.astype(jnp.bfloat16), preferred_element_type=jnp.float32)
        for part in e_parts
    ).reshape(heads, n_q, answer_len, blocks)
    sel = onehot.astype(jnp.bfloat16)
    e_slot = sum(
        jnp.einsum("hqtp,qpj->qhtj", part, sel, preferred_element_type=jnp.float32)
        for part in _split_terms(e_pass, 2)
    )
    m_loc = jnp.swapaxes(m_loc, 0, 1)
    l_loc = jnp.swapaxes(l_loc, 0, 1)
    o_loc = jnp.transpose(o_h.reshape(heads, n_q, answer_len, HS), (1, 2, 0, 3))

    n_local_q = n_q // n_dp
    def split_q(a):
        return a.reshape((nz, nx, n_local_q) + a.shape[1:])
    state = jax.tree.map(split_q, (m_loc, l_loc, o_loc, e_slot))
    state = _reduce_ring(state, 1, xi, nx, xf, xb)
    if nz & (nz - 1) == 0:
        state = _halving(state, zi, nz, lambda b: [(z * nx + x, (z ^ b) * nx + x) for z in range(nz) for x in range(nx)])
    else:
        state = _reduce_ring(state, 0, zi, nz, zf, zb)
    m_fin, l_fin, o_fin, e_fin = state
    context = o_fin / jnp.swapaxes(l_fin, -1, -2)[..., None]
    context = context.reshape(n_local_q, answer_len, inner).astype(jnp.bfloat16)
    mass = jnp.sum(e_fin / l_fin[..., None], axis=(1, 2)) / answer_len
    mass = lax.psum(mass, ("section", "mp"))
    return (context, mass)


def solution(mesh):
    nz, nx = _plane_shape(mesh)
    in_specs = (
        P("dp", None, None),
        P(),
        P("dp", ("section", "mp")),
        P("dp", ("section", "mp")),
        P("dp"),
        P(),
        P("dp", None, ("section", "mp")),
    )
    out_specs = (P("dp", None, ("section", "mp")), P("dp", None))

    def body(*args):
        return _local(nz, nx, *args)

    return jax.shard_map(body, mesh=mesh, in_specs=in_specs, out_specs=out_specs, check_vma=False)
```

```python
import os

import jax
import jax.numpy as jnp
from jax import lax
from jax.experimental import pallas as pl
from jax.sharding import PartitionSpec as P

HS = 64
WIRE = jnp.bfloat16


INTERPRET = os.environ.get("SOL_INTERPRET") == "1"
ROW_TILE = 1024


def _attn_kernel(q_ref, k_ref, v_ref, live_ref, blk_ref, m_ref, l_ref, o_ref, ep_ref):
    q = q_ref[0]
    k = k_ref[0]
    v = v_ref[0]
    live = live_ref[...] > 0
    s = lax.dot_general(q, k, (((1,), (1,)), ((), ())), preferred_element_type=jnp.float32)
    m = jnp.max(jnp.where(live, s, -jnp.inf), axis=1, keepdims=True)
    e = jnp.where(live, jnp.exp(s - m), 0.0)
    l = jnp.sum(e, axis=1, keepdims=True)
    e_hi = e.astype(jnp.bfloat16)
    e_lo = (e - e_hi.astype(jnp.float32)).astype(jnp.bfloat16)
    blk = blk_ref[...]
    o = jnp.dot(e_hi, v, preferred_element_type=jnp.float32) + jnp.dot(e_lo, v, preferred_element_type=jnp.float32)
    ep = jnp.dot(e_hi, blk, preferred_element_type=jnp.float32) + jnp.dot(e_lo, blk, preferred_element_type=jnp.float32)
    m_ref[0] = m
    l_ref[0] = l
    o_ref[0] = o
    ep_ref[0] = ep


def _attention(q_h, k_h, v_h, live_rows, block_of):
    heads, n_rows, hs = q_h.shape
    n_ps = k_h.shape[1]
    n_blk = block_of.shape[1]
    tile = ROW_TILE if n_rows % ROW_TILE == 0 else n_rows
    grid = (heads, n_rows // tile)
    row = lambda h, i: (h, i, 0)
    return pl.pallas_call(
        _attn_kernel,
        grid=grid,
        in_specs=[
            pl.BlockSpec((1, tile, hs), row),
            pl.BlockSpec((1, n_ps, hs), lambda h, i: (h, 0, 0)),
            pl.BlockSpec((1, n_ps, hs), lambda h, i: (h, 0, 0)),
            pl.BlockSpec((tile, n_ps), lambda h, i: (i, 0)),
            pl.BlockSpec((n_ps, n_blk), lambda h, i: (0, 0)),
        ],
        out_specs=[
            pl.BlockSpec((1, tile, 1), row),
            pl.BlockSpec((1, tile, 1), row),
            pl.BlockSpec((1, tile, hs), row),
            pl.BlockSpec((1, tile, n_blk), row),
        ],
        out_shape=[
            jax.ShapeDtypeStruct((heads, n_rows, 1), jnp.float32),
            jax.ShapeDtypeStruct((heads, n_rows, 1), jnp.float32),
            jax.ShapeDtypeStruct((heads, n_rows, hs), jnp.float32),
            jax.ShapeDtypeStruct((heads, n_rows, n_blk), jnp.float32),
        ],
        interpret=INTERPRET,
    )(q_h, k_h, v_h, live_rows, block_of)


def _plane_shape(mesh):
    n_dp = mesh.shape["dp"]
    try:
        xs = {d.coords[0] for d in mesh.devices[0, :, 0]}
        nx = len(xs)
    except Exception:
        nx = 2 if n_dp % 2 == 0 else 1
    return n_dp // nx, nx


def _ring_perm(nz, nx, along, step):
    pairs = []
    for z in range(nz):
        for x in range(nx):
            if along == "x":
                dst = z * nx + (x + step) % nx
            else:
                dst = ((z + step) % nz) * nx + x
            pairs.append((z * nx + x, dst))
    return pairs


def _gather_ring(block, n, fwd, bwd):
    if n == 1:
        return block[None]
    rel = [None] * n
    rel[0] = block
    f = block
    g = block
    for k in range(1, (n - 1) // 2 + 1):
        f = lax.ppermute(f, "dp", fwd)
        g = lax.ppermute(g, "dp", bwd)
        rel[n - k] = f
        rel[k] = g
    if n % 2 == 0:
        half = n // 2
        if block.shape[0] >= 2:
            cut = block.shape[0] // 2
            a = lax.ppermute(f[:cut], "dp", fwd)
            b = lax.ppermute(g[cut:], "dp", bwd)
            rel[half] = jnp.concatenate([a, b], axis=0)
        else:
            rel[half] = lax.ppermute(f, "dp", fwd)
    return jnp.stack(rel)


def _combine(a, b):
    ma, la, oa, ea = a
    mb, lb, ob, eb = b
    m = jnp.maximum(ma, mb)
    sa = jnp.where(ma == m, 1.0, jnp.exp(ma - m))
    sb = jnp.where(mb == m, 1.0, jnp.exp(mb - m))
    l = sa * la + sb * lb
    sa_o = jnp.swapaxes(sa, -1, -2)[..., None]
    sb_o = jnp.swapaxes(sb, -1, -2)[..., None]
    o = oa * sa_o + ob * sb_o
    e = ea * sa[..., None] + eb * sb[..., None]
    return (m, l, o, e)


def _split_terms(a, terms):
    big = jnp.float32(3.38e38)
    head = lax.reduce_precision(jnp.clip(a, -big, big), exponent_bits=8, mantissa_bits=7)
    head = jnp.where(jnp.isinf(a), a, head)
    out = [head.astype(WIRE)]
    rest = jnp.where(jnp.isinf(a), 0.0, a - head)
    for _ in range(terms - 1):
        t = lax.reduce_precision(rest, exponent_bits=8, mantissa_bits=7)
        out.append(t.astype(WIRE))
        rest = rest - t
    return out


def _to_wire(s):
    m, l, o, e = s
    lead = m.shape[:-2]
    parts = _split_terms(m, 3) + _split_terms(l, 2) + [o.astype(WIRE), e.astype(WIRE)]
    return jnp.concatenate([p.reshape(lead + (-1,)) for p in parts], axis=-1)


def _from_wire(w, shapes):
    m_shape, o_shape, e_shape = shapes
    lead = w.shape[:-1]
    n_m = 1
    for d in m_shape:
        n_m *= d
    n_o = 1
    for d in o_shape:
        n_o *= d
    pieces = []
    at = 0
    for size in (n_m, n_m, n_m, n_m, n_m, n_o):
        pieces.append(w[..., at:at + size].astype(jnp.float32))
        at += size
    pieces.append(w[..., at:].astype(jnp.float32))
    m = (pieces[0] + pieces[1]) + pieces[2]
    l = pieces[3] + pieces[4]
    return (
        m.reshape(lead + m_shape),
        l.reshape(lead + m_shape),
        pieces[5].reshape(lead + o_shape),
        pieces[6].reshape(lead + e_shape),
    )


def _shapes(s):
    m, l, o, e = s
    return (m.shape[-2:], o.shape[-3:], e.shape[-3:])


def _xfer(s, perm):
    return _from_wire(lax.ppermute(_to_wire(s), "dp", perm), _shapes(s))


def _halving(state, me, n, perm_of):
    bit = 1
    while bit < n:
        size = state[0].shape[0]
        mine = (me // bit) % 2
        pairs = jax.tree.map(lambda a: a.reshape((size // 2, 2) + a.shape[1:]), state)
        keep = jax.tree.map(lambda a: lax.dynamic_index_in_dim(a, mine, 1, keepdims=False), pairs)
        give = jax.tree.map(lambda a: lax.dynamic_index_in_dim(a, 1 - mine, 1, keepdims=False), pairs)
        state = _combine(keep, _xfer(give, perm_of(bit)))
        bit *= 2
    return jax.tree.map(lambda a: a[0], state)


def _reduce_ring(state, axis, me, n, fwd, bwd):
    def chunk(r):
        idx = (me + r) % n
        return jax.tree.map(lambda a: lax.dynamic_index_in_dim(a, idx, axis, keepdims=False), state)

    if n == 1:
        return chunk(0)
    nb = n // 2
    nf = n - 1 - nb
    bacc = chunk(n - nb)
    facc = None
    result = None
    for k in range(1, nb + 1):
        if nf > 0 and k == nb - nf + 1:
            facc = chunk(nf)
        recv_b = _xfer(bacc, bwd)
        recv_f = _xfer(facc, fwd) if facc is not None else None
        if k < nb:
            bacc = _combine(recv_b, chunk((k - nb) % n))
            if recv_f is not None:
                facc = _combine(recv_f, chunk(nb - k))
        else:
            result = _combine(chunk(0), recv_b)
            if recv_f is not None:
                result = _combine(result, recv_f)
    return result


def _local(nz, nx, states, norm_gain, key_weight, value_weight, pass_len, retrieval, queries):
    blocks, tokens, model_width = states.shape
    inner = key_weight.shape[1]
    heads = inner // HS
    rows_here = key_weight.shape[0]
    n_dp = nz * nx
    dpi = lax.axis_index("dp")
    zi = dpi // nx
    xi = dpi % nx
    xf = _ring_perm(nz, nx, "x", 1)
    xb = _ring_perm(nz, nx, "x", -1)
    zf = _ring_perm(nz, nx, "z", 1)
    zb = _ring_perm(nz, nx, "z", -1)

    n_lq, answer_len, _ = queries.shape
    q_rows = queries.reshape(-1, 2 * inner)
    wkv = jnp.concatenate([key_weight, value_weight], axis=1)
    wkv = jnp.concatenate([wkv, q_rows], axis=0)
    wx = _gather_ring(wkv, nx, xf, xb)
    wzx = _gather_ring(wx, nz, zf, zb)
    q_rel = wzx[:, :, rows_here:, :].reshape(nz, nx, n_lq, answer_len, inner)
    q_rel = jnp.roll(jnp.roll(q_rel, zi, axis=0), xi, axis=1)
    q_all = q_rel.reshape(n_dp * n_lq, answer_len, inner)
    wzx = wzx[:, :, :rows_here, :]

    widened = states.astype(jnp.float32)
    mean_square = jnp.mean(widened * widened, axis=-1, keepdims=True)
    normed = (widened * lax.rsqrt(mean_square + 1e-06) * norm_gain).astype(jnp.bfloat16)
    flat = normed.reshape(blocks * tokens, nz, nx, rows_here)
    flat = jnp.roll(flat, -zi, axis=1)
    flat = jnp.roll(flat, -xi, axis=2)
    kv = jnp.dot(
        flat.reshape(blocks * tokens, model_width),
        wzx.reshape(model_width, 2 * inner),
        preferred_element_type=jnp.float32,
    ).astype(jnp.bfloat16)
    keys = kv[:, :inner].reshape(blocks, tokens, heads, HS)
    values = kv[:, inner:].reshape(blocks, tokens, heads, HS)

    n_q = q_all.shape[0]
    n_ps = blocks * tokens
    q_h = jnp.swapaxes(q_all.reshape(n_q * answer_len, heads, HS), 0, 1)
    k_h = jnp.swapaxes(keys.reshape(n_ps, heads, HS), 0, 1)
    v_h = jnp.swapaxes(values.reshape(n_ps, heads, HS), 0, 1)
    local_ids = retrieval - dpi * blocks
    owned = (local_ids >= 0) & (local_ids < blocks)
    onehot = (local_ids[:, None, :] == jnp.arange(blocks, dtype=jnp.int32)[None, :, None]) & owned[:, None, :]
    picked = jnp.any(onehot, axis=2)
    positions = jnp.arange(tokens, dtype=jnp.int32)
    live = picked[:, :, None] & (positions[None, None, :] < pass_len[None, :, None])
    live_rows = jnp.broadcast_to(live.reshape(n_q, 1, n_ps), (n_q, answer_len, n_ps))
    live_rows = live_rows.reshape(n_q * answer_len, n_ps).astype(jnp.bfloat16)
    block_of = (jnp.arange(n_ps, dtype=jnp.int32)[:, None] // tokens) == jnp.arange(blocks, dtype=jnp.int32)[None, :]
    m_loc, l_loc, o_h, e_pass = _attention(q_h, k_h, v_h, live_rows, block_of.astype(jnp.bfloat16))
    m_loc = m_loc.reshape(heads, n_q, answer_len)
    l_loc = l_loc.reshape(heads, n_q, answer_len)
    e_pass = e_pass.reshape(heads, n_q, answer_len, blocks)
    sel = onehot.astype(jnp.bfloat16)
    e_slot = sum(
        jnp.einsum("hqtp,qpj->qhtj", part, sel, preferred_element_type=jnp.float32)
        for part in _split_terms(e_pass, 2)
    )
    m_loc = jnp.swapaxes(m_loc, 0, 1)
    l_loc = jnp.swapaxes(l_loc, 0, 1)
    o_loc = jnp.transpose(o_h.reshape(heads, n_q, answer_len, HS), (1, 2, 0, 3))

    n_local_q = n_q // n_dp
    def split_q(a):
        return a.reshape((nz, nx, n_local_q) + a.shape[1:])
    state = jax.tree.map(split_q, (m_loc, l_loc, o_loc, e_slot))
    state = _reduce_ring(state, 1, xi, nx, xf, xb)
    if nz & (nz - 1) == 0:
        state = _halving(state, zi, nz, lambda b: [(z * nx + x, (z ^ b) * nx + x) for z in range(nz) for x in range(nx)])
    else:
        state = _reduce_ring(state, 0, zi, nz, zf, zb)
    m_fin, l_fin, o_fin, e_fin = state
    context = o_fin / jnp.swapaxes(l_fin, -1, -2)[..., None]
    context = context.reshape(n_local_q, answer_len, inner).astype(jnp.bfloat16)
    mass = jnp.sum(e_fin / l_fin[..., None], axis=(1, 2)) / answer_len
    mass = lax.psum(mass, ("section", "mp"))
    return (context, mass)


def solution(mesh):
    nz, nx = _plane_shape(mesh)
    in_specs = (
        P("dp", None, None),
        P(),
        P("dp", ("section", "mp")),
        P("dp", ("section", "mp")),
        P("dp"),
        P(),
        P("dp", None, ("section", "mp")),
    )
    out_specs = (P("dp", None, ("section", "mp")), P("dp", None))

    def body(*args):
        return _local(nz, nx, *args)

    return jax.shard_map(body, mesh=mesh, in_specs=in_specs, out_specs=out_specs, check_vma=False)
```

```python
import os

import jax
import jax.numpy as jnp
from jax import lax
from jax.experimental import pallas as pl
from jax.sharding import PartitionSpec as P

HS = 64
WIRE = jnp.bfloat16


INTERPRET = os.environ.get("SOL_INTERPRET") == "1"
ROW_TILE = 1024


def _attn_kernel(q_ref, k_ref, v_ref, live_ref, blk_ref, o_ref, aux_ref):
    q = q_ref[0]
    k = k_ref[0]
    v = v_ref[0]
    live = live_ref[...] > 0
    s = lax.dot_general(q, k, (((1,), (1,)), ((), ())), preferred_element_type=jnp.float32)
    m = jnp.max(jnp.where(live, s, -jnp.inf), axis=1, keepdims=True)
    e = jnp.where(live, jnp.exp(s - m), 0.0)
    e_hi = e.astype(jnp.bfloat16)
    e_lo = (e - e_hi.astype(jnp.float32)).astype(jnp.bfloat16)
    blk = blk_ref[...]
    o = jnp.dot(e_hi, v, preferred_element_type=jnp.float32) + jnp.dot(e_lo, v, preferred_element_type=jnp.float32)
    aux = jnp.dot(e_hi, blk, preferred_element_type=jnp.float32) + jnp.dot(e_lo, blk, preferred_element_type=jnp.float32)
    col = lax.broadcasted_iota(jnp.int32, aux.shape, 1)
    o_ref[0] = o
    aux_ref[0] = jnp.where(col == aux.shape[1] - 1, m, aux)


def _attention(q_h, k_h, v_h, live_rows, block_of):
    heads, n_rows, hs = q_h.shape
    n_ps = k_h.shape[1]
    n_blk = block_of.shape[1]
    tile = ROW_TILE if n_rows % ROW_TILE == 0 else n_rows
    grid = (heads, n_rows // tile)
    row = lambda h, i: (h, i, 0)
    return pl.pallas_call(
        _attn_kernel,
        grid=grid,
        in_specs=[
            pl.BlockSpec((1, tile, hs), row),
            pl.BlockSpec((1, n_ps, hs), lambda h, i: (h, 0, 0)),
            pl.BlockSpec((1, n_ps, hs), lambda h, i: (h, 0, 0)),
            pl.BlockSpec((tile, n_ps), lambda h, i: (i, 0)),
            pl.BlockSpec((n_ps, n_blk), lambda h, i: (0, 0)),
        ],
        out_specs=[
            pl.BlockSpec((1, tile, hs), row),
            pl.BlockSpec((1, tile, n_blk), row),
        ],
        out_shape=[
            jax.ShapeDtypeStruct((heads, n_rows, hs), jnp.float32),
            jax.ShapeDtypeStruct((heads, n_rows, n_blk), jnp.float32),
        ],
        interpret=INTERPRET,
    )(q_h, k_h, v_h, live_rows, block_of)


def _plane_shape(mesh):
    n_dp = mesh.shape["dp"]
    try:
        xs = {d.coords[0] for d in mesh.devices[0, :, 0]}
        nx = len(xs)
    except Exception:
        nx = 2 if n_dp % 2 == 0 else 1
    return n_dp // nx, nx


def _ring_perm(nz, nx, along, step):
    pairs = []
    for z in range(nz):
        for x in range(nx):
            if along == "x":
                dst = z * nx + (x + step) % nx
            else:
                dst = ((z + step) % nz) * nx + x
            pairs.append((z * nx + x, dst))
    return pairs


def _gather_ring(block, n, fwd, bwd):
    if n == 1:
        return block[None]
    rel = [None] * n
    rel[0] = block
    f = block
    g = block
    for k in range(1, (n - 1) // 2 + 1):
        f = lax.ppermute(f, "dp", fwd)
        g = lax.ppermute(g, "dp", bwd)
        rel[n - k] = f
        rel[k] = g
    if n % 2 == 0:
        half = n // 2
        if block.shape[0] >= 2:
            cut = block.shape[0] // 2
            a = lax.ppermute(f[:cut], "dp", fwd)
            b = lax.ppermute(g[cut:], "dp", bwd)
            rel[half] = jnp.concatenate([a, b], axis=0)
        else:
            rel[half] = lax.ppermute(f, "dp", fwd)
    return jnp.stack(rel)


def _combine(a, b):
    ma, la, oa, ea = a
    mb, lb, ob, eb = b
    m = jnp.maximum(ma, mb)
    sa = jnp.where(ma == m, 1.0, jnp.exp(ma - m))
    sb = jnp.where(mb == m, 1.0, jnp.exp(mb - m))
    l = sa * la + sb * lb
    o = oa * sa[..., None] + ob * sb[..., None]
    e = ea * sa[..., None] + eb * sb[..., None]
    return (m, l, o, e)


def _split_terms(a, terms):
    big = jnp.float32(3.38e38)
    head = lax.reduce_precision(jnp.clip(a, -big, big), exponent_bits=8, mantissa_bits=7)
    head = jnp.where(jnp.isinf(a), a, head)
    out = [head.astype(WIRE)]
    rest = jnp.where(jnp.isinf(a), 0.0, a - head)
    for _ in range(terms - 1):
        t = lax.reduce_precision(rest, exponent_bits=8, mantissa_bits=7)
        out.append(t.astype(WIRE))
        rest = rest - t
    return out


def _to_wire(s):
    m, l, o, e = s
    lead = m.shape[:-2]
    parts = _split_terms(m, 3) + _split_terms(l, 2) + [o.astype(WIRE), e.astype(WIRE)]
    return jnp.concatenate([p.reshape(lead + (-1,)) for p in parts], axis=-1)


def _from_wire(w, shapes):
    m_shape, o_shape, e_shape = shapes
    lead = w.shape[:-1]
    n_m = 1
    for d in m_shape:
        n_m *= d
    n_o = 1
    for d in o_shape:
        n_o *= d
    pieces = []
    at = 0
    for size in (n_m, n_m, n_m, n_m, n_m, n_o):
        pieces.append(w[..., at:at + size].astype(jnp.float32))
        at += size
    pieces.append(w[..., at:].astype(jnp.float32))
    m = (pieces[0] + pieces[1]) + pieces[2]
    l = pieces[3] + pieces[4]
    return (
        m.reshape(lead + m_shape),
        l.reshape(lead + m_shape),
        pieces[5].reshape(lead + o_shape),
        pieces[6].reshape(lead + e_shape),
    )


def _shapes(s):
    m, l, o, e = s
    return (m.shape[-2:], o.shape[-3:], e.shape[-3:])


def _xfer(s, perm):
    return _from_wire(lax.ppermute(_to_wire(s), "dp", perm), _shapes(s))


def _halving(state, me, n, perm_of):
    bit = 1
    while bit < n:
        size = state[0].shape[0]
        mine = (me // bit) % 2
        pairs = jax.tree.map(lambda a: a.reshape((size // 2, 2) + a.shape[1:]), state)
        keep = jax.tree.map(lambda a: lax.dynamic_index_in_dim(a, mine, 1, keepdims=False), pairs)
        give = jax.tree.map(lambda a: lax.dynamic_index_in_dim(a, 1 - mine, 1, keepdims=False), pairs)
        state = _combine(keep, _xfer(give, perm_of(bit)))
        bit *= 2
    return jax.tree.map(lambda a: a[0], state)


def _reduce_ring(state, axis, me, n, fwd, bwd):
    def chunk(r):
        idx = (me + r) % n
        return jax.tree.map(lambda a: lax.dynamic_index_in_dim(a, idx, axis, keepdims=False), state)

    if n == 1:
        return chunk(0)
    nb = n // 2
    nf = n - 1 - nb
    bacc = chunk(n - nb)
    facc = None
    result = None
    for k in range(1, nb + 1):
        if nf > 0 and k == nb - nf + 1:
            facc = chunk(nf)
        recv_b = _xfer(bacc, bwd)
        recv_f = _xfer(facc, fwd) if facc is not None else None
        if k < nb:
            bacc = _combine(recv_b, chunk((k - nb) % n))
            if recv_f is not None:
                facc = _combine(recv_f, chunk(nb - k))
        else:
            result = _combine(chunk(0), recv_b)
            if recv_f is not None:
                result = _combine(result, recv_f)
    return result


def _local(nz, nx, states, norm_gain, key_weight, value_weight, pass_len, retrieval, queries):
    blocks, tokens, model_width = states.shape
    inner = key_weight.shape[1]
    heads = inner // HS
    rows_here = key_weight.shape[0]
    n_dp = nz * nx
    dpi = lax.axis_index("dp")
    zi = dpi // nx
    xi = dpi % nx
    xf = _ring_perm(nz, nx, "x", 1)
    xb = _ring_perm(nz, nx, "x", -1)
    zf = _ring_perm(nz, nx, "z", 1)
    zb = _ring_perm(nz, nx, "z", -1)

    n_lq, answer_len, _ = queries.shape
    q_rows = queries.reshape(-1, 2 * inner)
    wkv = jnp.concatenate([key_weight, value_weight], axis=1)
    wkv = jnp.concatenate([wkv, q_rows], axis=0)
    wx = _gather_ring(wkv, nx, xf, xb)
    wzx = _gather_ring(wx, nz, zf, zb)
    q_rel = wzx[:, :, rows_here:, :].reshape(nz, nx, n_lq, answer_len, inner)
    q_rel = jnp.roll(jnp.roll(q_rel, zi, axis=0), xi, axis=1)
    q_all = q_rel.reshape(n_dp * n_lq, answer_len, inner)
    wzx = wzx[:, :, :rows_here, :]

    widened = states.astype(jnp.float32)
    mean_square = jnp.mean(widened * widened, axis=-1, keepdims=True)
    normed = (widened * lax.rsqrt(mean_square + 1e-06) * norm_gain).astype(jnp.bfloat16)
    flat = normed.reshape(blocks * tokens, nz, nx, rows_here)
    flat = jnp.roll(flat, -zi, axis=1)
    flat = jnp.roll(flat, -xi, axis=2)
    kv = jnp.dot(
        flat.reshape(blocks * tokens, model_width),
        wzx.reshape(model_width, 2 * inner),
        preferred_element_type=jnp.float32,
    ).astype(jnp.bfloat16)
    keys = kv[:, :inner].reshape(blocks, tokens, heads, HS)
    values = kv[:, inner:].reshape(blocks, tokens, heads, HS)

    n_q = q_all.shape[0]
    n_ps = blocks * tokens
    q_h = jnp.swapaxes(q_all.reshape(n_q * answer_len, heads, HS), 0, 1)
    k_h = jnp.swapaxes(keys.reshape(n_ps, heads, HS), 0, 1)
    v_h = jnp.swapaxes(values.reshape(n_ps, heads, HS), 0, 1)
    local_ids = retrieval - dpi * blocks
    owned = (local_ids >= 0) & (local_ids < blocks)
    onehot = (local_ids[:, None, :] == jnp.arange(blocks, dtype=jnp.int32)[None, :, None]) & owned[:, None, :]
    picked = jnp.any(onehot, axis=2)
    positions = jnp.arange(tokens, dtype=jnp.int32)
    live = picked[:, :, None] & (positions[None, None, :] < pass_len[None, :, None])
    live_rows = jnp.broadcast_to(live.reshape(n_q, 1, n_ps), (n_q, answer_len, n_ps))
    live_rows = live_rows.reshape(n_q * answer_len, n_ps).astype(jnp.bfloat16)
    width = -(-(blocks + 2) // 128) * 128
    cols = jnp.arange(width, dtype=jnp.int32)[None, :]
    ps_block = jnp.arange(n_ps, dtype=jnp.int32)[:, None] // tokens
    block_of = ((ps_block == cols) | (cols == blocks)).astype(jnp.bfloat16)
    o_h, aux = _attention(q_h, k_h, v_h, live_rows, block_of)
    aux = aux.reshape(heads, n_q, answer_len, width)
    e_pass = aux[..., :blocks]
    l_loc = aux[..., blocks]
    m_loc = aux[..., width - 1]
    sel = onehot.astype(jnp.bfloat16)
    e_slot = sum(
        jnp.einsum("hqtp,qpj->qhtj", part, sel, preferred_element_type=jnp.float32)
        for part in _split_terms(e_pass, 2)
    )
    m_loc = jnp.swapaxes(m_loc, 0, 1)
    l_loc = jnp.swapaxes(l_loc, 0, 1)
    o_loc = jnp.swapaxes(o_h.reshape(heads, n_q, answer_len, HS), 0, 1)

    n_local_q = n_q // n_dp
    def split_q(a):
        return a.reshape((nz, nx, n_local_q) + a.shape[1:])
    state = jax.tree.map(split_q, (m_loc, l_loc, o_loc, e_slot))
    state = _reduce_ring(state, 1, xi, nx, xf, xb)
    if nz & (nz - 1) == 0:
        state = _halving(state, zi, nz, lambda b: [(z * nx + x, (z ^ b) * nx + x) for z in range(nz) for x in range(nx)])
    else:
        state = _reduce_ring(state, 0, zi, nz, zf, zb)
    m_fin, l_fin, o_fin, e_fin = state
    context = jnp.swapaxes(o_fin / l_fin[..., None], 1, 2)
    context = context.reshape(n_local_q, answer_len, inner).astype(jnp.bfloat16)
    mass = jnp.sum(e_fin / l_fin[..., None], axis=(1, 2)) / answer_len
    mass = lax.psum(mass, ("section", "mp"))
    return (context, mass)


def solution(mesh):
    nz, nx = _plane_shape(mesh)
    in_specs = (
        P("dp", None, None),
        P(),
        P("dp", ("section", "mp")),
        P("dp", ("section", "mp")),
        P("dp"),
        P(),
        P("dp", None, ("section", "mp")),
    )
    out_specs = (P("dp", None, ("section", "mp")), P("dp", None))

    def body(*args):
        return _local(nz, nx, *args)

    return jax.shard_map(body, mesh=mesh, in_specs=in_specs, out_specs=out_specs, check_vma=False)
```

```python
import os

import jax
import jax.numpy as jnp
from jax import lax
from jax.experimental import pallas as pl
from jax.sharding import PartitionSpec as P

HS = 64
WIRE = jnp.bfloat16


INTERPRET = os.environ.get("SOL_INTERPRET") == "1"
ROW_TILE = 1024


def _attn_kernel(q_ref, k_ref, v_ref, live_ref, blk_ref, o_ref, aux_ref):
    q = q_ref[0]
    k = k_ref[0]
    v = v_ref[0]
    live = live_ref[...] > 0
    s = lax.dot_general(q, k, (((1,), (1,)), ((), ())), preferred_element_type=jnp.float32)
    m = jnp.max(jnp.where(live, s, -jnp.inf), axis=1, keepdims=True)
    e = jnp.where(live, jnp.exp(s - m), 0.0)
    e_hi = e.astype(jnp.bfloat16)
    e_lo = (e - e_hi.astype(jnp.float32)).astype(jnp.bfloat16)
    blk = blk_ref[...]
    o = jnp.dot(e_hi, v, preferred_element_type=jnp.float32) + jnp.dot(e_lo, v, preferred_element_type=jnp.float32)
    aux = jnp.dot(e_hi, blk, preferred_element_type=jnp.float32) + jnp.dot(e_lo, blk, preferred_element_type=jnp.float32)
    col = lax.broadcasted_iota(jnp.int32, aux.shape, 1)
    o_ref[0] = o
    aux_ref[0] = jnp.where(col == aux.shape[1] - 1, m, aux)


def _attention(q_h, k_h, v_h, live_rows, block_of):
    heads, n_rows, hs = q_h.shape
    n_ps = k_h.shape[1]
    n_blk = block_of.shape[1]
    tile = ROW_TILE if n_rows % ROW_TILE == 0 else n_rows
    grid = (heads, n_rows // tile)
    row = lambda h, i: (h, i, 0)
    return pl.pallas_call(
        _attn_kernel,
        grid=grid,
        in_specs=[
            pl.BlockSpec((1, tile, hs), row),
            pl.BlockSpec((1, n_ps, hs), lambda h, i: (h, 0, 0)),
            pl.BlockSpec((1, n_ps, hs), lambda h, i: (h, 0, 0)),
            pl.BlockSpec((tile, n_ps), lambda h, i: (i, 0)),
            pl.BlockSpec((n_ps, n_blk), lambda h, i: (0, 0)),
        ],
        out_specs=[
            pl.BlockSpec((1, tile, hs), row),
            pl.BlockSpec((1, tile, n_blk), row),
        ],
        out_shape=[
            jax.ShapeDtypeStruct((heads, n_rows, hs), jnp.float32),
            jax.ShapeDtypeStruct((heads, n_rows, n_blk), jnp.float32),
        ],
        interpret=INTERPRET,
    )(q_h, k_h, v_h, live_rows, block_of)


def _plane_shape(mesh):
    n_dp = mesh.shape["dp"]
    try:
        xs = {d.coords[0] for d in mesh.devices[0, :, 0]}
        nx = len(xs)
    except Exception:
        nx = 2 if n_dp % 2 == 0 else 1
    return n_dp // nx, nx


def _ring_perm(nz, nx, along, step):
    pairs = []
    for z in range(nz):
        for x in range(nx):
            if along == "x":
                dst = z * nx + (x + step) % nx
            else:
                dst = ((z + step) % nz) * nx + x
            pairs.append((z * nx + x, dst))
    return pairs


def _gather_ring(block, n, fwd, bwd):
    if n == 1:
        return block[None]
    rel = [None] * n
    rel[0] = block
    f = block
    g = block
    for k in range(1, (n - 1) // 2 + 1):
        f = lax.ppermute(f, "dp", fwd)
        g = lax.ppermute(g, "dp", bwd)
        rel[n - k] = f
        rel[k] = g
    if n % 2 == 0:
        half = n // 2
        if block.shape[0] >= 2:
            cut = block.shape[0] // 2
            a = lax.ppermute(f[:cut], "dp", fwd)
            b = lax.ppermute(g[cut:], "dp", bwd)
            rel[half] = jnp.concatenate([a, b], axis=0)
        else:
            rel[half] = lax.ppermute(f, "dp", fwd)
    return jnp.stack(rel)


def _combine(a, b):
    ma, la, oa, ea = a
    mb, lb, ob, eb = b
    m = jnp.maximum(ma, mb)
    sa = jnp.where(ma == m, 1.0, jnp.exp(ma - m))
    sb = jnp.where(mb == m, 1.0, jnp.exp(mb - m))
    l = sa * la + sb * lb
    o = oa * sa[..., None] + ob * sb[..., None]
    e = ea * sa[..., None] + eb * sb[..., None]
    return (m, l, o, e)


def _split_terms(a, terms):
    big = jnp.float32(3.38e38)
    head = lax.reduce_precision(jnp.clip(a, -big, big), exponent_bits=8, mantissa_bits=7)
    head = jnp.where(jnp.isinf(a), a, head)
    out = [head.astype(WIRE)]
    rest = jnp.where(jnp.isinf(a), 0.0, a - head)
    for _ in range(terms - 1):
        t = lax.reduce_precision(rest, exponent_bits=8, mantissa_bits=7)
        out.append(t.astype(WIRE))
        rest = rest - t
    return out


def _to_wire(s):
    m, l, o, e = s
    lead = m.shape[:-2]
    parts = _split_terms(m, 3) + _split_terms(l, 2) + [o.astype(WIRE), e.astype(WIRE)]
    return jnp.concatenate([p.reshape(lead + (-1,)) for p in parts], axis=-1)


def _from_wire(w, shapes):
    m_shape, o_shape, e_shape = shapes
    lead = w.shape[:-1]
    n_m = 1
    for d in m_shape:
        n_m *= d
    n_o = 1
    for d in o_shape:
        n_o *= d
    pieces = []
    at = 0
    for size in (n_m, n_m, n_m, n_m, n_m, n_o):
        pieces.append(w[..., at:at + size].astype(jnp.float32))
        at += size
    pieces.append(w[..., at:].astype(jnp.float32))
    m = (pieces[0] + pieces[1]) + pieces[2]
    l = pieces[3] + pieces[4]
    return (
        m.reshape(lead + m_shape),
        l.reshape(lead + m_shape),
        pieces[5].reshape(lead + o_shape),
        pieces[6].reshape(lead + e_shape),
    )


def _shapes(s):
    m, l, o, e = s
    return (m.shape[-2:], o.shape[-3:], e.shape[-3:])


def _xfer(s, perm):
    return _from_wire(lax.ppermute(_to_wire(s), "dp", perm), _shapes(s))


def _halving(state, me, n, perm_of):
    bit = 1
    while bit < n:
        size = state[0].shape[0]
        mine = (me // bit) % 2
        pairs = jax.tree.map(lambda a: a.reshape((size // 2, 2) + a.shape[1:]), state)
        keep = jax.tree.map(lambda a: lax.dynamic_index_in_dim(a, mine, 1, keepdims=False), pairs)
        give = jax.tree.map(lambda a: lax.dynamic_index_in_dim(a, 1 - mine, 1, keepdims=False), pairs)
        state = _combine(keep, _xfer(give, perm_of(bit)))
        bit *= 2
    return jax.tree.map(lambda a: a[0], state)


def _reduce_ring(state, axis, me, n, fwd, bwd, chunk_fn=None):
    def chunk(r):
        if chunk_fn is not None:
            return chunk_fn(r)
        idx = (me + r) % n
        return jax.tree.map(lambda a: lax.dynamic_index_in_dim(a, idx, axis, keepdims=False), state)

    if n == 1:
        return chunk(0)
    nb = n // 2
    nf = n - 1 - nb
    bacc = chunk(n - nb)
    facc = None
    result = None
    for k in range(1, nb + 1):
        if nf > 0 and k == nb - nf + 1:
            facc = chunk(nf)
        recv_b = _xfer(bacc, bwd)
        recv_f = _xfer(facc, fwd) if facc is not None else None
        if k < nb:
            bacc = _combine(recv_b, chunk((k - nb) % n))
            if recv_f is not None:
                facc = _combine(recv_f, chunk(nb - k))
        else:
            result = _combine(chunk(0), recv_b)
            if recv_f is not None:
                result = _combine(result, recv_f)
    return result


def _local(nz, nx, states, norm_gain, key_weight, value_weight, pass_len, retrieval, queries):
    blocks, tokens, model_width = states.shape
    inner = key_weight.shape[1]
    heads = inner // HS
    rows_here = key_weight.shape[0]
    n_dp = nz * nx
    dpi = lax.axis_index("dp")
    zi = dpi // nx
    xi = dpi % nx
    xf = _ring_perm(nz, nx, "x", 1)
    xb = _ring_perm(nz, nx, "x", -1)
    zf = _ring_perm(nz, nx, "z", 1)
    zb = _ring_perm(nz, nx, "z", -1)

    n_lq, answer_len, _ = queries.shape
    q_rows = queries.reshape(-1, 2 * inner)
    wkv = jnp.concatenate([key_weight, value_weight], axis=1)
    wkv = jnp.concatenate([wkv, q_rows], axis=0)
    wx = _gather_ring(wkv, nx, xf, xb)
    wzx = _gather_ring(wx, nz, zf, zb)
    q_rel = wzx[:, :, rows_here:, :].reshape(nz, nx, n_lq, answer_len, inner)
    q_rel = jnp.roll(jnp.roll(q_rel, zi, axis=0), xi, axis=1)
    q_grp = jnp.swapaxes(q_rel, 0, 1)
    wzx = wzx[:, :, :rows_here, :]

    widened = states.astype(jnp.float32)
    mean_square = jnp.mean(widened * widened, axis=-1, keepdims=True)
    normed = (widened * lax.rsqrt(mean_square + 1e-06) * norm_gain).astype(jnp.bfloat16)
    flat = normed.reshape(blocks * tokens, nz, nx, rows_here)
    flat = jnp.roll(flat, -zi, axis=1)
    flat = jnp.roll(flat, -xi, axis=2)
    kv = jnp.dot(
        flat.reshape(blocks * tokens, model_width),
        wzx.reshape(model_width, 2 * inner),
        preferred_element_type=jnp.float32,
    ).astype(jnp.bfloat16)
    keys = kv[:, :inner].reshape(blocks, tokens, heads, HS)
    values = kv[:, inner:].reshape(blocks, tokens, heads, HS)

    n_local_q = n_lq
    n_ps = blocks * tokens
    k_h = jnp.swapaxes(keys.reshape(n_ps, heads, HS), 0, 1)
    v_h = jnp.swapaxes(values.reshape(n_ps, heads, HS), 0, 1)
    width = -(-(blocks + 2) // 128) * 128
    cols = jnp.arange(width, dtype=jnp.int32)[None, :]
    ps_block = jnp.arange(n_ps, dtype=jnp.int32)[:, None] // tokens
    block_of = ((ps_block == cols) | (cols == blocks)).astype(jnp.bfloat16)
    positions = jnp.arange(tokens, dtype=jnp.int32)
    ret_grp = jnp.swapaxes(retrieval.reshape(nz, nx, n_lq, -1), 0, 1)

    def owner_state(r):
        xq = (xi + r) % nx
        q_c = lax.dynamic_index_in_dim(q_grp, xq, 0, keepdims=False)
        ret_c = lax.dynamic_index_in_dim(ret_grp, xq, 0, keepdims=False).reshape(nz * n_lq, -1)
        n_c = nz * n_lq
        q_h = jnp.swapaxes(q_c.reshape(n_c * answer_len, heads, HS), 0, 1)
        local_ids = ret_c - dpi * blocks
        owned = (local_ids >= 0) & (local_ids < blocks)
        onehot = (local_ids[:, None, :] == jnp.arange(blocks, dtype=jnp.int32)[None, :, None]) & owned[:, None, :]
        picked = jnp.any(onehot, axis=2)
        live = picked[:, :, None] & (positions[None, None, :] < pass_len[None, :, None])
        live_rows = jnp.broadcast_to(live.reshape(n_c, 1, n_ps), (n_c, answer_len, n_ps))
        live_rows = live_rows.reshape(n_c * answer_len, n_ps).astype(jnp.bfloat16)
        o_h, aux = _attention(q_h, k_h, v_h, live_rows, block_of)
        aux = aux.reshape(heads, n_c, answer_len, width)
        e_pass = aux[..., :blocks]
        l_c = jnp.swapaxes(aux[..., blocks], 0, 1)
        m_c = jnp.swapaxes(aux[..., width - 1], 0, 1)
        sel = onehot.astype(jnp.bfloat16)
        e_c = sum(
            jnp.einsum("hqtp,qpj->qhtj", part, sel, preferred_element_type=jnp.float32)
            for part in _split_terms(e_pass, 2)
        )
        o_c = jnp.swapaxes(o_h.reshape(heads, n_c, answer_len, HS), 0, 1)
        split = lambda a: a.reshape((nz, n_lq) + a.shape[1:])
        return jax.tree.map(split, (m_c, l_c, o_c, e_c))

    state = _reduce_ring(None, 1, xi, nx, xf, xb, chunk_fn=owner_state)
    if nz & (nz - 1) == 0:
        state = _halving(state, zi, nz, lambda b: [(z * nx + x, (z ^ b) * nx + x) for z in range(nz) for x in range(nx)])
    else:
        state = _reduce_ring(state, 0, zi, nz, zf, zb)
    m_fin, l_fin, o_fin, e_fin = state
    context = jnp.swapaxes(o_fin / l_fin[..., None], 1, 2)
    context = context.reshape(n_local_q, answer_len, inner).astype(jnp.bfloat16)
    mass = jnp.sum(e_fin / l_fin[..., None], axis=(1, 2)) / answer_len
    mass = lax.psum(mass, ("section", "mp"))
    return (context, mass)


def solution(mesh):
    nz, nx = _plane_shape(mesh)
    in_specs = (
        P("dp", None, None),
        P(),
        P("dp", ("section", "mp")),
        P("dp", ("section", "mp")),
        P("dp"),
        P(),
        P("dp", None, ("section", "mp")),
    )
    out_specs = (P("dp", None, ("section", "mp")), P("dp", None))

    def body(*args):
        return _local(nz, nx, *args)

    return jax.shard_map(body, mesh=mesh, in_specs=in_specs, out_specs=out_specs, check_vma=False)
```

```python
import os

import jax
import jax.numpy as jnp
from jax import lax
from jax.experimental import pallas as pl
from jax.sharding import PartitionSpec as P

HS = 64
WIRE = jnp.bfloat16


INTERPRET = os.environ.get("SOL_INTERPRET") == "1"
ROW_TILE = 1024


def _attn_kernel(q_ref, k_ref, v_ref, live_ref, blk_ref, o_ref, aux_ref):
    q = q_ref[0]
    k = k_ref[0]
    v = v_ref[0]
    live = live_ref[...] > 0
    s = lax.dot_general(q, k, (((1,), (1,)), ((), ())), preferred_element_type=jnp.float32)
    m = jnp.max(jnp.where(live, s, -jnp.inf), axis=1, keepdims=True)
    e = jnp.where(live, jnp.exp(s - m), 0.0)
    e_hi = e.astype(jnp.bfloat16)
    e_lo = (e - e_hi.astype(jnp.float32)).astype(jnp.bfloat16)
    blk = blk_ref[...]
    o = jnp.dot(e_hi, v, preferred_element_type=jnp.float32) + jnp.dot(e_lo, v, preferred_element_type=jnp.float32)
    aux = jnp.dot(e_hi, blk, preferred_element_type=jnp.float32) + jnp.dot(e_lo, blk, preferred_element_type=jnp.float32)
    col = lax.broadcasted_iota(jnp.int32, aux.shape, 1)
    o_ref[0] = o
    aux_ref[0] = jnp.where(col == aux.shape[1] - 1, m, aux)


def _attention(q_h, k_h, v_h, live_rows, block_of):
    heads, n_rows, hs = q_h.shape
    n_ps = k_h.shape[1]
    n_blk = block_of.shape[1]
    tile = ROW_TILE if n_rows % ROW_TILE == 0 else n_rows
    grid = (heads, n_rows // tile)
    row = lambda h, i: (h, i, 0)
    return pl.pallas_call(
        _attn_kernel,
        grid=grid,
        in_specs=[
            pl.BlockSpec((1, tile, hs), row),
            pl.BlockSpec((1, n_ps, hs), lambda h, i: (h, 0, 0)),
            pl.BlockSpec((1, n_ps, hs), lambda h, i: (h, 0, 0)),
            pl.BlockSpec((tile, n_ps), lambda h, i: (i, 0)),
            pl.BlockSpec((n_ps, n_blk), lambda h, i: (0, 0)),
        ],
        out_specs=[
            pl.BlockSpec((1, tile, hs), row),
            pl.BlockSpec((1, tile, n_blk), row),
        ],
        out_shape=[
            jax.ShapeDtypeStruct((heads, n_rows, hs), jnp.float32),
            jax.ShapeDtypeStruct((heads, n_rows, n_blk), jnp.float32),
        ],
        interpret=INTERPRET,
    )(q_h, k_h, v_h, live_rows, block_of)


def _plane_shape(mesh):
    n_dp = mesh.shape["dp"]
    try:
        xs = {d.coords[0] for d in mesh.devices[0, :, 0]}
        nx = len(xs)
    except Exception:
        nx = 2 if n_dp % 2 == 0 else 1
    return n_dp // nx, nx


def _ring_perm(nz, nx, along, step):
    pairs = []
    for z in range(nz):
        for x in range(nx):
            if along == "x":
                dst = z * nx + (x + step) % nx
            else:
                dst = ((z + step) % nz) * nx + x
            pairs.append((z * nx + x, dst))
    return pairs


def _gather_ring(block, n, fwd, bwd):
    if n == 1:
        return block[None]
    rel = [None] * n
    rel[0] = block
    f = block
    g = block
    for k in range(1, (n - 1) // 2 + 1):
        f = lax.ppermute(f, "dp", fwd)
        g = lax.ppermute(g, "dp", bwd)
        rel[n - k] = f
        rel[k] = g
    if n % 2 == 0:
        half = n // 2
        if block.shape[0] >= 2:
            cut = block.shape[0] // 2
            a = lax.ppermute(f[:cut], "dp", fwd)
            b = lax.ppermute(g[cut:], "dp", bwd)
            rel[half] = jnp.concatenate([a, b], axis=0)
        else:
            rel[half] = lax.ppermute(f, "dp", fwd)
    return jnp.stack(rel)


def _combine(a, b):
    ma, la, oa, ea = a
    mb, lb, ob, eb = b
    m = jnp.maximum(ma, mb)
    sa = jnp.where(ma == m, 1.0, jnp.exp(ma - m))
    sb = jnp.where(mb == m, 1.0, jnp.exp(mb - m))
    l = sa * la + sb * lb
    o = oa * sa[..., None] + ob * sb[..., None]
    e = ea * sa[..., None] + eb * sb[..., None]
    return (m, l, o, e)


def _split_terms(a, terms):
    big = jnp.float32(3.38e38)
    head = lax.reduce_precision(jnp.clip(a, -big, big), exponent_bits=8, mantissa_bits=7)
    head = jnp.where(jnp.isinf(a), a, head)
    out = [head.astype(WIRE)]
    rest = jnp.where(jnp.isinf(a), 0.0, a - head)
    for _ in range(terms - 1):
        t = lax.reduce_precision(rest, exponent_bits=8, mantissa_bits=7)
        out.append(t.astype(WIRE))
        rest = rest - t
    return out


def _to_wire(s):
    m, l, o, e = s
    lead = m.shape[:-2]
    parts = _split_terms(m, 3) + _split_terms(l, 2) + [o.astype(WIRE), e.astype(WIRE)]
    return jnp.concatenate([p.reshape(lead + (-1,)) for p in parts], axis=-1)


def _from_wire(w, shapes):
    m_shape, o_shape, e_shape = shapes
    lead = w.shape[:-1]
    n_m = 1
    for d in m_shape:
        n_m *= d
    n_o = 1
    for d in o_shape:
        n_o *= d
    pieces = []
    at = 0
    for size in (n_m, n_m, n_m, n_m, n_m, n_o):
        pieces.append(w[..., at:at + size].astype(jnp.float32))
        at += size
    pieces.append(w[..., at:].astype(jnp.float32))
    m = (pieces[0] + pieces[1]) + pieces[2]
    l = pieces[3] + pieces[4]
    return (
        m.reshape(lead + m_shape),
        l.reshape(lead + m_shape),
        pieces[5].reshape(lead + o_shape),
        pieces[6].reshape(lead + e_shape),
    )


def _shapes(s):
    m, l, o, e = s
    return (m.shape[-2:], o.shape[-3:], e.shape[-3:])


def _xfer(s, perm):
    return _from_wire(lax.ppermute(_to_wire(s), "dp", perm), _shapes(s))


def _halving(state, me, n, perm_of):
    bit = 1
    while bit < n:
        size = state[0].shape[0]
        mine = (me // bit) % 2
        pairs = jax.tree.map(lambda a: a.reshape((size // 2, 2) + a.shape[1:]), state)
        keep = jax.tree.map(lambda a: lax.dynamic_index_in_dim(a, mine, 1, keepdims=False), pairs)
        give = jax.tree.map(lambda a: lax.dynamic_index_in_dim(a, 1 - mine, 1, keepdims=False), pairs)
        state = _combine(keep, _xfer(give, perm_of(bit)))
        bit *= 2
    return jax.tree.map(lambda a: a[0], state)


def _reduce_ring(state, axis, me, n, fwd, bwd):
    def chunk(r):
        idx = (me + r) % n
        return jax.tree.map(lambda a: lax.dynamic_index_in_dim(a, idx, axis, keepdims=False), state)

    if n == 1:
        return chunk(0)
    nb = n // 2
    nf = n - 1 - nb
    bacc = chunk(n - nb)
    facc = None
    result = None
    for k in range(1, nb + 1):
        if nf > 0 and k == nb - nf + 1:
            facc = chunk(nf)
        recv_b = _xfer(bacc, bwd)
        recv_f = _xfer(facc, fwd) if facc is not None else None
        if k < nb:
            bacc = _combine(recv_b, chunk((k - nb) % n))
            if recv_f is not None:
                facc = _combine(recv_f, chunk(nb - k))
        else:
            result = _combine(chunk(0), recv_b)
            if recv_f is not None:
                result = _combine(result, recv_f)
    return result


def _local(nz, nx, states, norm_gain, key_weight, value_weight, pass_len, retrieval, queries):
    blocks, tokens, model_width = states.shape
    inner = key_weight.shape[1]
    heads = inner // HS
    rows_here = key_weight.shape[0]
    n_dp = nz * nx
    dpi = lax.axis_index("dp")
    zi = dpi // nx
    xi = dpi % nx
    xf = _ring_perm(nz, nx, "x", 1)
    xb = _ring_perm(nz, nx, "x", -1)
    zf = _ring_perm(nz, nx, "z", 1)
    zb = _ring_perm(nz, nx, "z", -1)

    n_lq, answer_len, _ = queries.shape
    q_rows = queries.reshape(-1, 2 * inner)
    wkv = jnp.concatenate([key_weight, value_weight], axis=1)
    wkv = jnp.concatenate([wkv, q_rows], axis=0)
    wx = _gather_ring(wkv, nx, xf, xb)
    wzx = _gather_ring(wx, nz, zf, zb)
    q_rel = wzx[:, :, rows_here:, :].reshape(nz, nx, n_lq, answer_len, inner)
    q_rel = jnp.roll(jnp.roll(q_rel, zi, axis=0), xi, axis=1)
    q_all = q_rel.reshape(n_dp * n_lq, answer_len, inner)
    wzx = wzx[:, :, :rows_here, :]

    widened = states.astype(jnp.float32)
    mean_square = jnp.mean(widened * widened, axis=-1, keepdims=True)
    normed = (widened * lax.rsqrt(mean_square + 1e-06) * norm_gain).astype(jnp.bfloat16)
    flat = normed.reshape(blocks * tokens, nz, nx, rows_here)
    flat = jnp.roll(flat, -zi, axis=1)
    flat = jnp.roll(flat, -xi, axis=2)
    kv = jnp.dot(
        flat.reshape(blocks * tokens, model_width),
        wzx.reshape(model_width, 2 * inner),
        preferred_element_type=jnp.float32,
    ).astype(jnp.bfloat16)
    keys = kv[:, :inner].reshape(blocks, tokens, heads, HS)
    values = kv[:, inner:].reshape(blocks, tokens, heads, HS)

    n_q = q_all.shape[0]
    n_ps = blocks * tokens
    q_h = jnp.swapaxes(q_all.reshape(n_q * answer_len, heads, HS), 0, 1)
    k_h = jnp.swapaxes(keys.reshape(n_ps, heads, HS), 0, 1)
    v_h = jnp.swapaxes(values.reshape(n_ps, heads, HS), 0, 1)
    local_ids = retrieval - dpi * blocks
    owned = (local_ids >= 0) & (local_ids < blocks)
    onehot = (local_ids[:, None, :] == jnp.arange(blocks, dtype=jnp.int32)[None, :, None]) & owned[:, None, :]
    picked = jnp.any(onehot, axis=2)
    positions = jnp.arange(tokens, dtype=jnp.int32)
    live = picked[:, :, None] & (positions[None, None, :] < pass_len[None, :, None])
    live_rows = jnp.broadcast_to(live.reshape(n_q, 1, n_ps), (n_q, answer_len, n_ps))
    live_rows = live_rows.reshape(n_q * answer_len, n_ps).astype(jnp.bfloat16)
    width = -(-(blocks + 2) // 128) * 128
    cols = jnp.arange(width, dtype=jnp.int32)[None, :]
    ps_block = jnp.arange(n_ps, dtype=jnp.int32)[:, None] // tokens
    block_of = ((ps_block == cols) | (cols == blocks)).astype(jnp.bfloat16)
    o_h, aux = _attention(q_h, k_h, v_h, live_rows, block_of)
    aux = aux.reshape(heads, n_q, answer_len, width)
    e_pass = aux[..., :blocks]
    l_loc = aux[..., blocks]
    m_loc = aux[..., width - 1]
    m_loc = jnp.swapaxes(m_loc, 0, 1)
    l_loc = jnp.swapaxes(l_loc, 0, 1)
    o_loc = jnp.swapaxes(o_h.reshape(heads, n_q, answer_len, HS), 0, 1)
    mine_x = (jnp.arange(nx, dtype=jnp.int32) == xi).astype(jnp.float32)
    e_own = jnp.swapaxes(e_pass, 0, 1)[..., None, :] * mine_x[:, None]
    e_own = e_own.reshape(e_own.shape[:3] + (nx * blocks,))

    n_local_q = n_q // n_dp
    def split_q(a):
        return a.reshape((nz, nx, n_local_q) + a.shape[1:])
    state = jax.tree.map(split_q, (m_loc, l_loc, o_loc, e_own))
    state = _reduce_ring(state, 1, xi, nx, xf, xb)
    m_x, l_x, o_x, e_x = state
    ret_c = lax.dynamic_index_in_dim(retrieval.reshape(nz, nx, n_local_q, -1), xi, 1, keepdims=False)
    cand = (zi * nx + jnp.arange(nx, dtype=jnp.int32))[:, None] * blocks + jnp.arange(blocks, dtype=jnp.int32)[None, :]
    to_slot = (ret_c[:, :, None, :] == cand.reshape(1, 1, nx * blocks, 1)).astype(jnp.bfloat16)
    e_x = sum(
        jnp.einsum("zqhtk,zqkj->zqhtj", part, to_slot, preferred_element_type=jnp.float32)
        for part in _split_terms(e_x, 2)
    )
    state = (m_x, l_x, o_x, e_x)
    if nz & (nz - 1) == 0:
        state = _halving(state, zi, nz, lambda b: [(z * nx + x, (z ^ b) * nx + x) for z in range(nz) for x in range(nx)])
    else:
        state = _reduce_ring(state, 0, zi, nz, zf, zb)
    m_fin, l_fin, o_fin, e_fin = state
    context = jnp.swapaxes(o_fin / l_fin[..., None], 1, 2)
    context = context.reshape(n_local_q, answer_len, inner).astype(jnp.bfloat16)
    mass = jnp.sum(e_fin / l_fin[..., None], axis=(1, 2)) / answer_len
    mass = lax.psum(mass, ("section", "mp"))
    return (context, mass)


def solution(mesh):
    nz, nx = _plane_shape(mesh)
    in_specs = (
        P("dp", None, None),
        P(),
        P("dp", ("section", "mp")),
        P("dp", ("section", "mp")),
        P("dp"),
        P(),
        P("dp", None, ("section", "mp")),
    )
    out_specs = (P("dp", None, ("section", "mp")), P("dp", None))

    def body(*args):
        return _local(nz, nx, *args)

    return jax.shard_map(body, mesh=mesh, in_specs=in_specs, out_specs=out_specs, check_vma=False)
```

```python
import os

import jax
import jax.numpy as jnp
from jax import lax
from jax.experimental import pallas as pl
from jax.sharding import PartitionSpec as P

HS = 64
WIRE = jnp.bfloat16


INTERPRET = os.environ.get("SOL_INTERPRET") == "1"
ROW_TILE = 1024


def _attn_kernel(q_ref, k_ref, v_ref, live_ref, blk_ref, o_ref, aux_ref):
    q = q_ref[0]
    k = k_ref[0]
    v = v_ref[0]
    live = live_ref[...] > 0
    s = lax.dot_general(q, k, (((1,), (1,)), ((), ())), preferred_element_type=jnp.float32)
    m = jnp.max(jnp.where(live, s, -jnp.inf), axis=1, keepdims=True)
    e = jnp.where(live, jnp.exp(s - m), 0.0)
    e_hi = e.astype(jnp.bfloat16)
    e_lo = (e - e_hi.astype(jnp.float32)).astype(jnp.bfloat16)
    blk = blk_ref[...]
    o = jnp.dot(e_hi, v, preferred_element_type=jnp.float32) + jnp.dot(e_lo, v, preferred_element_type=jnp.float32)
    aux = jnp.dot(e_hi, blk, preferred_element_type=jnp.float32) + jnp.dot(e_lo, blk, preferred_element_type=jnp.float32)
    col = lax.broadcasted_iota(jnp.int32, aux.shape, 1)
    o_ref[0] = o
    aux_ref[0] = jnp.where(col == aux.shape[1] - 1, m, aux)


def _attention(q_h, k_h, v_h, live_rows, block_of):
    heads, n_rows, hs = q_h.shape
    n_ps = k_h.shape[1]
    n_blk = block_of.shape[1]
    tile = ROW_TILE if n_rows % ROW_TILE == 0 else n_rows
    grid = (heads, n_rows // tile)
    row = lambda h, i: (h, i, 0)
    return pl.pallas_call(
        _attn_kernel,
        grid=grid,
        in_specs=[
            pl.BlockSpec((1, tile, hs), row),
            pl.BlockSpec((1, n_ps, hs), lambda h, i: (h, 0, 0)),
            pl.BlockSpec((1, n_ps, hs), lambda h, i: (h, 0, 0)),
            pl.BlockSpec((tile, n_ps), lambda h, i: (i, 0)),
            pl.BlockSpec((n_ps, n_blk), lambda h, i: (0, 0)),
        ],
        out_specs=[
            pl.BlockSpec((1, tile, hs), row),
            pl.BlockSpec((1, tile, n_blk), row),
        ],
        out_shape=[
            jax.ShapeDtypeStruct((heads, n_rows, hs), jnp.float32),
            jax.ShapeDtypeStruct((heads, n_rows, n_blk), jnp.float32),
        ],
        interpret=INTERPRET,
    )(q_h, k_h, v_h, live_rows, block_of)


def _plane_shape(mesh):
    n_dp = mesh.shape["dp"]
    try:
        xs = {d.coords[0] for d in mesh.devices[0, :, 0]}
        nx = len(xs)
    except Exception:
        nx = 2 if n_dp % 2 == 0 else 1
    return n_dp // nx, nx


def _ring_perm(nz, nx, along, step):
    pairs = []
    for z in range(nz):
        for x in range(nx):
            if along == "x":
                dst = z * nx + (x + step) % nx
            else:
                dst = ((z + step) % nz) * nx + x
            pairs.append((z * nx + x, dst))
    return pairs


def _gather_ring(block, n, fwd, bwd):
    if n == 1:
        return block[None]
    rel = [None] * n
    rel[0] = block
    f = block
    g = block
    for k in range(1, (n - 1) // 2 + 1):
        f = lax.ppermute(f, "dp", fwd)
        g = lax.ppermute(g, "dp", bwd)
        rel[n - k] = f
        rel[k] = g
    if n % 2 == 0:
        half = n // 2
        if block.shape[0] >= 2:
            cut = block.shape[0] // 2
            a = lax.ppermute(f[:cut], "dp", fwd)
            b = lax.ppermute(g[cut:], "dp", bwd)
            rel[half] = jnp.concatenate([a, b], axis=0)
        else:
            rel[half] = lax.ppermute(f, "dp", fwd)
    return jnp.stack(rel)


def _combine(a, b):
    ma, la, oa, ea = a
    mb, lb, ob, eb = b
    m = jnp.maximum(ma, mb)
    sa = jnp.where(ma == m, 1.0, jnp.exp(ma - m))
    sb = jnp.where(mb == m, 1.0, jnp.exp(mb - m))
    l = sa * la + sb * lb
    o = oa * sa[..., None] + ob * sb[..., None]
    e = ea * sa[..., None] + eb * sb[..., None]
    return (m, l, o, e)


def _split_terms(a, terms):
    big = jnp.float32(3.38e38)
    head = lax.reduce_precision(jnp.clip(a, -big, big), exponent_bits=8, mantissa_bits=7)
    head = jnp.where(jnp.isinf(a), a, head)
    out = [head.astype(WIRE)]
    rest = jnp.where(jnp.isinf(a), 0.0, a - head)
    for _ in range(terms - 1):
        t = lax.reduce_precision(rest, exponent_bits=8, mantissa_bits=7)
        out.append(t.astype(WIRE))
        rest = rest - t
    return out


def _to_wire(s):
    m, l, o, e = s
    lead = m.shape[:-1]
    parts = _split_terms(m, 3) + _split_terms(l, 2) + [o.astype(WIRE), e.astype(WIRE)]
    return jnp.concatenate([p.reshape(lead + (-1,)) for p in parts], axis=-1)


def _from_wire(w, shapes):
    m_shape, o_shape, e_shape = shapes
    lead = w.shape[:-1]
    n_m = 1
    for d in m_shape:
        n_m *= d
    n_o = 1
    for d in o_shape:
        n_o *= d
    pieces = []
    at = 0
    for size in (n_m, n_m, n_m, n_m, n_m, n_o):
        pieces.append(w[..., at:at + size].astype(jnp.float32))
        at += size
    pieces.append(w[..., at:].astype(jnp.float32))
    m = (pieces[0] + pieces[1]) + pieces[2]
    l = pieces[3] + pieces[4]
    return (
        m.reshape(lead + m_shape),
        l.reshape(lead + m_shape),
        pieces[5].reshape(lead + o_shape),
        pieces[6].reshape(lead + e_shape),
    )


def _shapes(s):
    m, l, o, e = s
    return (m.shape[-1:], o.shape[-2:], e.shape[-2:])


def _xfer(s, perm):
    return _from_wire(lax.ppermute(_to_wire(s), "dp", perm), _shapes(s))


def _halving(state, me, n, perm_of):
    bit = 1
    while bit < n:
        size = state[0].shape[1]
        mine = (me // bit) % 2
        pairs = jax.tree.map(lambda a: a.reshape(a.shape[:1] + (size // 2, 2) + a.shape[2:]), state)
        keep = jax.tree.map(lambda a: lax.dynamic_index_in_dim(a, mine, 2, keepdims=False), pairs)
        give = jax.tree.map(lambda a: lax.dynamic_index_in_dim(a, 1 - mine, 2, keepdims=False), pairs)
        state = _combine(keep, _xfer(give, perm_of(bit)))
        bit *= 2
    return jax.tree.map(lambda a: a[:, 0], state)


def _reduce_ring(state, axis, me, n, fwd, bwd):
    def chunk(r):
        idx = (me + r) % n
        return jax.tree.map(lambda a: lax.dynamic_index_in_dim(a, idx, axis, keepdims=False), state)

    if n == 1:
        return chunk(0)
    nb = n // 2
    nf = n - 1 - nb
    bacc = chunk(n - nb)
    facc = None
    result = None
    for k in range(1, nb + 1):
        if nf > 0 and k == nb - nf + 1:
            facc = chunk(nf)
        recv_b = _xfer(bacc, bwd)
        recv_f = _xfer(facc, fwd) if facc is not None else None
        if k < nb:
            bacc = _combine(recv_b, chunk((k - nb) % n))
            if recv_f is not None:
                facc = _combine(recv_f, chunk(nb - k))
        else:
            result = _combine(chunk(0), recv_b)
            if recv_f is not None:
                result = _combine(result, recv_f)
    return result


def _local(nz, nx, states, norm_gain, key_weight, value_weight, pass_len, retrieval, queries):
    blocks, tokens, model_width = states.shape
    inner = key_weight.shape[1]
    heads = inner // HS
    rows_here = key_weight.shape[0]
    n_dp = nz * nx
    dpi = lax.axis_index("dp")
    zi = dpi // nx
    xi = dpi % nx
    xf = _ring_perm(nz, nx, "x", 1)
    xb = _ring_perm(nz, nx, "x", -1)
    zf = _ring_perm(nz, nx, "z", 1)
    zb = _ring_perm(nz, nx, "z", -1)

    n_lq, answer_len, _ = queries.shape
    q_rows = queries.reshape(-1, 2 * inner)
    wkv = jnp.concatenate([key_weight, value_weight], axis=1)
    wkv = jnp.concatenate([wkv, q_rows], axis=0)
    wx = _gather_ring(wkv, nx, xf, xb)
    wzx = _gather_ring(wx, nz, zf, zb)
    q_rel = wzx[:, :, rows_here:, :].reshape(nz, nx, n_lq, answer_len, inner)
    q_rel = jnp.roll(jnp.roll(q_rel, zi, axis=0), xi, axis=1)
    q_all = q_rel.reshape(n_dp * n_lq, answer_len, inner)
    wzx = wzx[:, :, :rows_here, :]

    widened = states.astype(jnp.float32)
    mean_square = jnp.mean(widened * widened, axis=-1, keepdims=True)
    normed = (widened * lax.rsqrt(mean_square + 1e-06) * norm_gain).astype(jnp.bfloat16)
    flat = normed.reshape(blocks * tokens, nz, nx, rows_here)
    flat = jnp.roll(flat, -zi, axis=1)
    flat = jnp.roll(flat, -xi, axis=2)
    kv = jnp.dot(
        flat.reshape(blocks * tokens, model_width),
        wzx.reshape(model_width, 2 * inner),
        preferred_element_type=jnp.float32,
    ).astype(jnp.bfloat16)
    keys = kv[:, :inner].reshape(blocks, tokens, heads, HS)
    values = kv[:, inner:].reshape(blocks, tokens, heads, HS)

    n_q = q_all.shape[0]
    n_ps = blocks * tokens
    q_h = jnp.swapaxes(q_all.reshape(n_q * answer_len, heads, HS), 0, 1)
    k_h = jnp.swapaxes(keys.reshape(n_ps, heads, HS), 0, 1)
    v_h = jnp.swapaxes(values.reshape(n_ps, heads, HS), 0, 1)
    local_ids = retrieval - dpi * blocks
    owned = (local_ids >= 0) & (local_ids < blocks)
    onehot = (local_ids[:, None, :] == jnp.arange(blocks, dtype=jnp.int32)[None, :, None]) & owned[:, None, :]
    picked = jnp.any(onehot, axis=2)
    positions = jnp.arange(tokens, dtype=jnp.int32)
    live = picked[:, :, None] & (positions[None, None, :] < pass_len[None, :, None])
    live_rows = jnp.broadcast_to(live.reshape(n_q, 1, n_ps), (n_q, answer_len, n_ps))
    live_rows = live_rows.reshape(n_q * answer_len, n_ps).astype(jnp.bfloat16)
    width = -(-(blocks + 2) // 128) * 128
    cols = jnp.arange(width, dtype=jnp.int32)[None, :]
    ps_block = jnp.arange(n_ps, dtype=jnp.int32)[:, None] // tokens
    block_of = ((ps_block == cols) | (cols == blocks)).astype(jnp.bfloat16)
    o_h, aux = _attention(q_h, k_h, v_h, live_rows, block_of)
    aux = aux.reshape(heads, n_q, answer_len, width)
    e_pass = aux[..., :blocks]
    l_loc = aux[..., blocks]
    m_loc = aux[..., width - 1]
    sel = onehot.astype(jnp.bfloat16)
    e_slot = sum(
        jnp.einsum("hqtp,qpj->hqtj", part, sel, preferred_element_type=jnp.float32)
        for part in _split_terms(e_pass, 2)
    )
    o_loc = o_h.reshape(heads, n_q, answer_len, HS)

    n_local_q = n_q // n_dp
    def split_q(a):
        return a.reshape(a.shape[:1] + (nz, nx, n_local_q) + a.shape[2:])
    state = jax.tree.map(split_q, (m_loc, l_loc, o_loc, e_slot))
    state = _reduce_ring(state, 2, xi, nx, xf, xb)
    if nz & (nz - 1) == 0:
        state = _halving(state, zi, nz, lambda b: [(z * nx + x, (z ^ b) * nx + x) for z in range(nz) for x in range(nx)])
    else:
        state = _reduce_ring(state, 1, zi, nz, zf, zb)
    m_fin, l_fin, o_fin, e_fin = state
    context = jnp.transpose(o_fin / l_fin[..., None], (1, 2, 0, 3))
    context = context.reshape(n_local_q, answer_len, inner).astype(jnp.bfloat16)
    mass = jnp.sum(e_fin / l_fin[..., None], axis=(0, 2)) / answer_len
    mass = lax.psum(mass, ("section", "mp"))
    return (context, mass)


def solution(mesh):
    nz, nx = _plane_shape(mesh)
    in_specs = (
        P("dp", None, None),
        P(),
        P("dp", ("section", "mp")),
        P("dp", ("section", "mp")),
        P("dp"),
        P(),
        P("dp", None, ("section", "mp")),
    )
    out_specs = (P("dp", None, ("section", "mp")), P("dp", None))

    def body(*args):
        return _local(nz, nx, *args)

    return jax.shard_map(body, mesh=mesh, in_specs=in_specs, out_specs=out_specs, check_vma=False)
```

```python
import os

import jax
import jax.numpy as jnp
from jax import lax
from jax.experimental import pallas as pl
from jax.sharding import PartitionSpec as P

HS = 64
WIRE = jnp.bfloat16


INTERPRET = os.environ.get("SOL_INTERPRET") == "1"
ROW_TILE = 1024


def _attn_kernel(q_ref, k_ref, v_ref, live_ref, blk_ref, o_ref, aux_ref):
    q = q_ref[0]
    k = k_ref[0]
    v = v_ref[0]
    live = live_ref[...] > 0
    s = lax.dot_general(q, k, (((1,), (1,)), ((), ())), preferred_element_type=jnp.float32)
    m = jnp.max(jnp.where(live, s, -jnp.inf), axis=1, keepdims=True)
    e = jnp.where(live, jnp.exp(s - m), 0.0)
    e_hi = e.astype(jnp.bfloat16)
    e_lo = (e - e_hi.astype(jnp.float32)).astype(jnp.bfloat16)
    blk = blk_ref[...]
    o = jnp.dot(e_hi, v, preferred_element_type=jnp.float32) + jnp.dot(e_lo, v, preferred_element_type=jnp.float32)
    aux = jnp.dot(e_hi, blk, preferred_element_type=jnp.float32) + jnp.dot(e_lo, blk, preferred_element_type=jnp.float32)
    col = lax.broadcasted_iota(jnp.int32, aux.shape, 1)
    o_ref[0] = o
    aux_ref[0] = jnp.where(col == aux.shape[1] - 1, m, aux)


def _attention(q_h, k_h, v_h, live_rows, block_of):
    heads, n_rows, hs = q_h.shape
    n_ps = k_h.shape[1]
    n_blk = block_of.shape[1]
    tile = ROW_TILE if n_rows % ROW_TILE == 0 else n_rows
    grid = (heads, n_rows // tile)
    row = lambda h, i: (h, i, 0)
    return pl.pallas_call(
        _attn_kernel,
        grid=grid,
        in_specs=[
            pl.BlockSpec((1, tile, hs), row),
            pl.BlockSpec((1, n_ps, hs), lambda h, i: (h, 0, 0)),
            pl.BlockSpec((1, n_ps, hs), lambda h, i: (h, 0, 0)),
            pl.BlockSpec((tile, n_ps), lambda h, i: (i, 0)),
            pl.BlockSpec((n_ps, n_blk), lambda h, i: (0, 0)),
        ],
        out_specs=[
            pl.BlockSpec((1, tile, hs), row),
            pl.BlockSpec((1, tile, n_blk), row),
        ],
        out_shape=[
            jax.ShapeDtypeStruct((heads, n_rows, hs), jnp.float32),
            jax.ShapeDtypeStruct((heads, n_rows, n_blk), jnp.float32),
        ],
        interpret=INTERPRET,
    )(q_h, k_h, v_h, live_rows, block_of)


def _plane_shape(mesh):
    n_dp = mesh.shape["dp"]
    try:
        xs = {d.coords[0] for d in mesh.devices[0, :, 0]}
        nx = len(xs)
    except Exception:
        nx = 2 if n_dp % 2 == 0 else 1
    return n_dp // nx, nx


def _ring_perm(nz, nx, along, step):
    pairs = []
    for z in range(nz):
        for x in range(nx):
            if along == "x":
                dst = z * nx + (x + step) % nx
            else:
                dst = ((z + step) % nz) * nx + x
            pairs.append((z * nx + x, dst))
    return pairs


def _gather_ring(block, n, fwd, bwd):
    if n == 1:
        return block[None]
    rel = [None] * n
    rel[0] = block
    f = block
    g = block
    for k in range(1, (n - 1) // 2 + 1):
        f = lax.ppermute(f, "dp", fwd)
        g = lax.ppermute(g, "dp", bwd)
        rel[n - k] = f
        rel[k] = g
    if n % 2 == 0:
        half = n // 2
        if block.shape[0] >= 2:
            cut = block.shape[0] // 2
            a = lax.ppermute(f[:cut], "dp", fwd)
            b = lax.ppermute(g[cut:], "dp", bwd)
            rel[half] = jnp.concatenate([a, b], axis=0)
        else:
            rel[half] = lax.ppermute(f, "dp", fwd)
    return jnp.stack(rel)


def _combine(a, b):
    ma, la, oa, ea = a
    mb, lb, ob, eb = b
    m = jnp.maximum(ma, mb)
    sa = jnp.where(ma == m, 1.0, jnp.exp(ma - m))
    sb = jnp.where(mb == m, 1.0, jnp.exp(mb - m))
    l = sa * la + sb * lb
    o = oa * sa[..., None] + ob * sb[..., None]
    e = ea * sa[..., None] + eb * sb[..., None]
    return (m, l, o, e)


def _split_terms(a, terms):
    big = jnp.float32(3.38e38)
    head = lax.reduce_precision(jnp.clip(a, -big, big), exponent_bits=8, mantissa_bits=7)
    head = jnp.where(jnp.isinf(a), a, head)
    out = [head.astype(WIRE)]
    rest = jnp.where(jnp.isinf(a), 0.0, a - head)
    for _ in range(terms - 1):
        t = lax.reduce_precision(rest, exponent_bits=8, mantissa_bits=7)
        out.append(t.astype(WIRE))
        rest = rest - t
    return out


def _to_wire(s):
    m, l, o, e = s
    lead = m.shape[:-1]
    parts = _split_terms(m, 3) + _split_terms(l, 2) + [o.astype(WIRE), e.astype(WIRE)]
    return jnp.concatenate([p.reshape(lead + (-1,)) for p in parts], axis=-1)


def _from_wire(w, shapes):
    m_shape, o_shape, e_shape = shapes
    lead = w.shape[:-1]
    n_m = 1
    for d in m_shape:
        n_m *= d
    n_o = 1
    for d in o_shape:
        n_o *= d
    pieces = []
    at = 0
    for size in (n_m, n_m, n_m, n_m, n_m, n_o):
        pieces.append(w[..., at:at + size].astype(jnp.float32))
        at += size
    pieces.append(w[..., at:].astype(jnp.float32))
    m = (pieces[0] + pieces[1]) + pieces[2]
    l = pieces[3] + pieces[4]
    return (
        m.reshape(lead + m_shape),
        l.reshape(lead + m_shape),
        pieces[5].reshape(lead + o_shape),
        pieces[6].reshape(lead + e_shape),
    )


def _shapes(s):
    m, l, o, e = s
    return (m.shape[-1:], o.shape[-2:], e.shape[-2:])


def _xfer(s, perm):
    return _from_wire(lax.ppermute(_to_wire(s), "dp", perm), _shapes(s))


def _halving(state, me, n, perm_of):
    bit = 1
    while bit < n:
        size = state[0].shape[1]
        mine = (me // bit) % 2
        pairs = jax.tree.map(lambda a: a.reshape(a.shape[:1] + (size // 2, 2) + a.shape[2:]), state)
        keep = jax.tree.map(lambda a: lax.dynamic_index_in_dim(a, mine, 2, keepdims=False), pairs)
        give = jax.tree.map(lambda a: lax.dynamic_index_in_dim(a, 1 - mine, 2, keepdims=False), pairs)
        state = _combine(keep, _xfer(give, perm_of(bit)))
        bit *= 2
    return jax.tree.map(lambda a: a[:, 0], state)


def _reduce_ring(state, axis, me, n, fwd, bwd):
    def chunk(r):
        idx = (me + r) % n
        return jax.tree.map(lambda a: lax.dynamic_index_in_dim(a, idx, axis, keepdims=False), state)

    if n == 1:
        return chunk(0)
    nb = n // 2
    nf = n - 1 - nb
    bacc = chunk(n - nb)
    facc = None
    result = None
    for k in range(1, nb + 1):
        if nf > 0 and k == nb - nf + 1:
            facc = chunk(nf)
        recv_b = _xfer(bacc, bwd)
        recv_f = _xfer(facc, fwd) if facc is not None else None
        if k < nb:
            bacc = _combine(recv_b, chunk((k - nb) % n))
            if recv_f is not None:
                facc = _combine(recv_f, chunk(nb - k))
        else:
            result = _combine(chunk(0), recv_b)
            if recv_f is not None:
                result = _combine(result, recv_f)
    return result


def _local(nz, nx, states, norm_gain, key_weight, value_weight, pass_len, retrieval, queries):
    blocks, tokens, model_width = states.shape
    inner = key_weight.shape[1]
    heads = inner // HS
    rows_here = key_weight.shape[0]
    n_dp = nz * nx
    dpi = lax.axis_index("dp")
    zi = dpi // nx
    xi = dpi % nx
    xf = _ring_perm(nz, nx, "x", 1)
    xb = _ring_perm(nz, nx, "x", -1)
    zf = _ring_perm(nz, nx, "z", 1)
    zb = _ring_perm(nz, nx, "z", -1)

    n_lq, answer_len, _ = queries.shape
    q_rows = queries.reshape(-1, 2 * inner)
    wkv = jnp.concatenate([key_weight, value_weight], axis=1)
    wkv = jnp.concatenate([wkv, q_rows], axis=0)
    wx = _gather_ring(wkv, nx, xf, xb)
    wzx = _gather_ring(wx, nz, zf, zb)
    q_rel = wzx[:, :, rows_here:, :].reshape(nz, nx, n_lq, answer_len, inner)
    q_rel = jnp.roll(jnp.roll(q_rel, zi, axis=0), xi, axis=1)
    q_all = q_rel.reshape(n_dp * n_lq, answer_len, inner)
    wzx = wzx[:, :, :rows_here, :]

    widened = states.astype(jnp.float32)
    mean_square = jnp.mean(widened * widened, axis=-1, keepdims=True)
    normed = (widened * lax.rsqrt(mean_square + 1e-06) * norm_gain).astype(jnp.bfloat16)
    flat = normed.reshape(blocks * tokens, nz, nx, rows_here)
    flat = jnp.roll(flat, -zi, axis=1)
    flat = jnp.roll(flat, -xi, axis=2)
    kv = jnp.dot(
        flat.reshape(blocks * tokens, model_width),
        wzx.reshape(model_width, 2 * inner),
        preferred_element_type=jnp.float32,
    ).astype(jnp.bfloat16)
    keys = kv[:, :inner].reshape(blocks, tokens, heads, HS)
    values = kv[:, inner:].reshape(blocks, tokens, heads, HS)

    n_q = q_all.shape[0]
    n_ps = blocks * tokens
    q_h = jnp.swapaxes(q_all.reshape(n_q * answer_len, heads, HS), 0, 1)
    k_h = jnp.swapaxes(keys.reshape(n_ps, heads, HS), 0, 1)
    v_h = jnp.swapaxes(values.reshape(n_ps, heads, HS), 0, 1)
    local_ids = retrieval - dpi * blocks
    owned = (local_ids >= 0) & (local_ids < blocks)
    onehot = (local_ids[:, None, :] == jnp.arange(blocks, dtype=jnp.int32)[None, :, None]) & owned[:, None, :]
    picked = jnp.any(onehot, axis=2)
    positions = jnp.arange(tokens, dtype=jnp.int32)
    live = picked[:, :, None] & (positions[None, None, :] < pass_len[None, :, None])
    live_rows = jnp.broadcast_to(live.reshape(n_q, 1, n_ps), (n_q, answer_len, n_ps))
    live_rows = live_rows.reshape(n_q * answer_len, n_ps).astype(jnp.bfloat16)
    width = -(-(blocks + 2) // 128) * 128
    cols = jnp.arange(width, dtype=jnp.int32)[None, :]
    ps_block = jnp.arange(n_ps, dtype=jnp.int32)[:, None] // tokens
    block_of = ((ps_block == cols) | (cols == blocks)).astype(jnp.bfloat16)
    o_h, aux = _attention(q_h, k_h, v_h, live_rows, block_of)
    aux = aux.reshape(heads, n_q, answer_len, width)
    e_pass = aux[..., :blocks]
    l_loc = aux[..., blocks]
    m_loc = aux[..., width - 1]
    sel = onehot.astype(jnp.float32)
    e_slot = jnp.sum(e_pass[..., :, None] * sel[None, :, None, :, :], axis=3)
    o_loc = o_h.reshape(heads, n_q, answer_len, HS)

    n_local_q = n_q // n_dp
    def split_q(a):
        return a.reshape(a.shape[:1] + (nz, nx, n_local_q) + a.shape[2:])
    state = jax.tree.map(split_q, (m_loc, l_loc, o_loc, e_slot))
    state = _reduce_ring(state, 2, xi, nx, xf, xb)
    if nz & (nz - 1) == 0:
        state = _halving(state, zi, nz, lambda b: [(z * nx + x, (z ^ b) * nx + x) for z in range(nz) for x in range(nx)])
    else:
        state = _reduce_ring(state, 1, zi, nz, zf, zb)
    m_fin, l_fin, o_fin, e_fin = state
    context = jnp.transpose(o_fin / l_fin[..., None], (1, 2, 0, 3))
    context = context.reshape(n_local_q, answer_len, inner).astype(jnp.bfloat16)
    mass = jnp.sum(e_fin / l_fin[..., None], axis=(0, 2)) / answer_len
    mass = lax.psum(mass, ("section", "mp"))
    return (context, mass)


def solution(mesh):
    nz, nx = _plane_shape(mesh)
    in_specs = (
        P("dp", None, None),
        P(),
        P("dp", ("section", "mp")),
        P("dp", ("section", "mp")),
        P("dp"),
        P(),
        P("dp", None, ("section", "mp")),
    )
    out_specs = (P("dp", None, ("section", "mp")), P("dp", None))

    def body(*args):
        return _local(nz, nx, *args)

    return jax.shard_map(body, mesh=mesh, in_specs=in_specs, out_specs=out_specs, check_vma=False)
```

```python
import os

import jax
import jax.numpy as jnp
from jax import lax
from jax.experimental import pallas as pl
from jax.sharding import PartitionSpec as P

HS = 64
WIRE = jnp.bfloat16


INTERPRET = os.environ.get("SOL_INTERPRET") == "1"
ROW_TILE = 2048


def _attn_kernel(q_ref, k_ref, v_ref, live_ref, blk_ref, o_ref, aux_ref):
    q = q_ref[0]
    k = k_ref[0]
    v = v_ref[0]
    live = live_ref[...] > 0
    s = lax.dot_general(q, k, (((1,), (1,)), ((), ())), preferred_element_type=jnp.float32)
    m = jnp.max(jnp.where(live, s, -jnp.inf), axis=1, keepdims=True)
    e = jnp.where(live, jnp.exp(s - m), 0.0)
    e_hi = e.astype(jnp.bfloat16)
    e_lo = (e - e_hi.astype(jnp.float32)).astype(jnp.bfloat16)
    blk = blk_ref[...]
    o = jnp.dot(e_hi, v, preferred_element_type=jnp.float32) + jnp.dot(e_lo, v, preferred_element_type=jnp.float32)
    aux = jnp.dot(e_hi, blk, preferred_element_type=jnp.float32) + jnp.dot(e_lo, blk, preferred_element_type=jnp.float32)
    col = lax.broadcasted_iota(jnp.int32, aux.shape, 1)
    o_ref[0] = o
    aux_ref[0] = jnp.where(col == aux.shape[1] - 1, m, aux)


def _attention(q_h, k_h, v_h, live_rows, block_of):
    heads, n_rows, hs = q_h.shape
    n_ps = k_h.shape[1]
    n_blk = block_of.shape[1]
    tile = ROW_TILE if n_rows % ROW_TILE == 0 else n_rows
    grid = (heads, n_rows // tile)
    row = lambda h, i: (h, i, 0)
    return pl.pallas_call(
        _attn_kernel,
        grid=grid,
        in_specs=[
            pl.BlockSpec((1, tile, hs), row),
            pl.BlockSpec((1, n_ps, hs), lambda h, i: (h, 0, 0)),
            pl.BlockSpec((1, n_ps, hs), lambda h, i: (h, 0, 0)),
            pl.BlockSpec((tile, n_ps), lambda h, i: (i, 0)),
            pl.BlockSpec((n_ps, n_blk), lambda h, i: (0, 0)),
        ],
        out_specs=[
            pl.BlockSpec((1, tile, hs), row),
            pl.BlockSpec((1, tile, n_blk), row),
        ],
        out_shape=[
            jax.ShapeDtypeStruct((heads, n_rows, hs), jnp.float32),
            jax.ShapeDtypeStruct((heads, n_rows, n_blk), jnp.float32),
        ],
        interpret=INTERPRET,
    )(q_h, k_h, v_h, live_rows, block_of)


def _plane_shape(mesh):
    n_dp = mesh.shape["dp"]
    try:
        xs = {d.coords[0] for d in mesh.devices[0, :, 0]}
        nx = len(xs)
    except Exception:
        nx = 2 if n_dp % 2 == 0 else 1
    return n_dp // nx, nx


def _ring_perm(nz, nx, along, step):
    pairs = []
    for z in range(nz):
        for x in range(nx):
            if along == "x":
                dst = z * nx + (x + step) % nx
            else:
                dst = ((z + step) % nz) * nx + x
            pairs.append((z * nx + x, dst))
    return pairs


def _gather_ring(block, n, fwd, bwd):
    if n == 1:
        return block[None]
    rel = [None] * n
    rel[0] = block
    f = block
    g = block
    for k in range(1, (n - 1) // 2 + 1):
        f = lax.ppermute(f, "dp", fwd)
        g = lax.ppermute(g, "dp", bwd)
        rel[n - k] = f
        rel[k] = g
    if n % 2 == 0:
        half = n // 2
        if block.shape[0] >= 2:
            cut = block.shape[0] // 2
            a = lax.ppermute(f[:cut], "dp", fwd)
            b = lax.ppermute(g[cut:], "dp", bwd)
            rel[half] = jnp.concatenate([a, b], axis=0)
        else:
            rel[half] = lax.ppermute(f, "dp", fwd)
    return jnp.stack(rel)


def _combine(a, b):
    ma, la, oa, ea = a
    mb, lb, ob, eb = b
    m = jnp.maximum(ma, mb)
    sa = jnp.where(ma == m, 1.0, jnp.exp(ma - m))
    sb = jnp.where(mb == m, 1.0, jnp.exp(mb - m))
    l = sa * la + sb * lb
    o = oa * sa[..., None] + ob * sb[..., None]
    e = ea * sa[..., None] + eb * sb[..., None]
    return (m, l, o, e)


def _split_terms(a, terms):
    big = jnp.float32(3.38e38)
    head = lax.reduce_precision(jnp.clip(a, -big, big), exponent_bits=8, mantissa_bits=7)
    head = jnp.where(jnp.isinf(a), a, head)
    out = [head.astype(WIRE)]
    rest = jnp.where(jnp.isinf(a), 0.0, a - head)
    for _ in range(terms - 1):
        t = lax.reduce_precision(rest, exponent_bits=8, mantissa_bits=7)
        out.append(t.astype(WIRE))
        rest = rest - t
    return out


def _to_wire(s):
    m, l, o, e = s
    lead = m.shape[:-1]
    parts = _split_terms(m, 3) + _split_terms(l, 2) + [o.astype(WIRE), e.astype(WIRE)]
    return jnp.concatenate([p.reshape(lead + (-1,)) for p in parts], axis=-1)


def _from_wire(w, shapes):
    m_shape, o_shape, e_shape = shapes
    lead = w.shape[:-1]
    n_m = 1
    for d in m_shape:
        n_m *= d
    n_o = 1
    for d in o_shape:
        n_o *= d
    pieces = []
    at = 0
    for size in (n_m, n_m, n_m, n_m, n_m, n_o):
        pieces.append(w[..., at:at + size].astype(jnp.float32))
        at += size
    pieces.append(w[..., at:].astype(jnp.float32))
    m = (pieces[0] + pieces[1]) + pieces[2]
    l = pieces[3] + pieces[4]
    return (
        m.reshape(lead + m_shape),
        l.reshape(lead + m_shape),
        pieces[5].reshape(lead + o_shape),
        pieces[6].reshape(lead + e_shape),
    )


def _shapes(s):
    m, l, o, e = s
    return (m.shape[-1:], o.shape[-2:], e.shape[-2:])


def _xfer(s, perm):
    return _from_wire(lax.ppermute(_to_wire(s), "dp", perm), _shapes(s))


def _halving(state, me, n, perm_of):
    bit = 1
    while bit < n:
        size = state[0].shape[1]
        mine = (me // bit) % 2
        pairs = jax.tree.map(lambda a: a.reshape(a.shape[:1] + (size // 2, 2) + a.shape[2:]), state)
        keep = jax.tree.map(lambda a: lax.dynamic_index_in_dim(a, mine, 2, keepdims=False), pairs)
        give = jax.tree.map(lambda a: lax.dynamic_index_in_dim(a, 1 - mine, 2, keepdims=False), pairs)
        state = _combine(keep, _xfer(give, perm_of(bit)))
        bit *= 2
    return jax.tree.map(lambda a: a[:, 0], state)


def _reduce_ring(state, axis, me, n, fwd, bwd):
    def chunk(r):
        idx = (me + r) % n
        return jax.tree.map(lambda a: lax.dynamic_index_in_dim(a, idx, axis, keepdims=False), state)

    if n == 1:
        return chunk(0)
    nb = n // 2
    nf = n - 1 - nb
    bacc = chunk(n - nb)
    facc = None
    result = None
    for k in range(1, nb + 1):
        if nf > 0 and k == nb - nf + 1:
            facc = chunk(nf)
        recv_b = _xfer(bacc, bwd)
        recv_f = _xfer(facc, fwd) if facc is not None else None
        if k < nb:
            bacc = _combine(recv_b, chunk((k - nb) % n))
            if recv_f is not None:
                facc = _combine(recv_f, chunk(nb - k))
        else:
            result = _combine(chunk(0), recv_b)
            if recv_f is not None:
                result = _combine(result, recv_f)
    return result


def _local(nz, nx, states, norm_gain, key_weight, value_weight, pass_len, retrieval, queries):
    blocks, tokens, model_width = states.shape
    inner = key_weight.shape[1]
    heads = inner // HS
    rows_here = key_weight.shape[0]
    n_dp = nz * nx
    dpi = lax.axis_index("dp")
    zi = dpi // nx
    xi = dpi % nx
    xf = _ring_perm(nz, nx, "x", 1)
    xb = _ring_perm(nz, nx, "x", -1)
    zf = _ring_perm(nz, nx, "z", 1)
    zb = _ring_perm(nz, nx, "z", -1)

    n_lq, answer_len, _ = queries.shape
    q_rows = queries.reshape(-1, 2 * inner)
    wkv = jnp.concatenate([key_weight, value_weight], axis=1)
    wkv = jnp.concatenate([wkv, q_rows], axis=0)
    wx = _gather_ring(wkv, nx, xf, xb)
    wzx = _gather_ring(wx, nz, zf, zb)
    q_rel = wzx[:, :, rows_here:, :].reshape(nz, nx, n_lq, answer_len, inner)
    q_rel = jnp.roll(jnp.roll(q_rel, zi, axis=0), xi, axis=1)
    q_all = q_rel.reshape(n_dp * n_lq, answer_len, inner)
    wzx = wzx[:, :, :rows_here, :]

    widened = states.astype(jnp.float32)
    mean_square = jnp.mean(widened * widened, axis=-1, keepdims=True)
    normed = (widened * lax.rsqrt(mean_square + 1e-06) * norm_gain).astype(jnp.bfloat16)
    flat = normed.reshape(blocks * tokens, nz, nx, rows_here)
    flat = jnp.roll(flat, -zi, axis=1)
    flat = jnp.roll(flat, -xi, axis=2)
    kv = jnp.dot(
        flat.reshape(blocks * tokens, model_width),
        wzx.reshape(model_width, 2 * inner),
        preferred_element_type=jnp.float32,
    ).astype(jnp.bfloat16)
    keys = kv[:, :inner].reshape(blocks, tokens, heads, HS)
    values = kv[:, inner:].reshape(blocks, tokens, heads, HS)

    n_q = q_all.shape[0]
    n_ps = blocks * tokens
    q_h = jnp.swapaxes(q_all.reshape(n_q * answer_len, heads, HS), 0, 1)
    k_h = jnp.swapaxes(keys.reshape(n_ps, heads, HS), 0, 1)
    v_h = jnp.swapaxes(values.reshape(n_ps, heads, HS), 0, 1)
    local_ids = retrieval - dpi * blocks
    owned = (local_ids >= 0) & (local_ids < blocks)
    onehot = (local_ids[:, None, :] == jnp.arange(blocks, dtype=jnp.int32)[None, :, None]) & owned[:, None, :]
    picked = jnp.any(onehot, axis=2)
    positions = jnp.arange(tokens, dtype=jnp.int32)
    live = picked[:, :, None] & (positions[None, None, :] < pass_len[None, :, None])
    live_rows = jnp.broadcast_to(live.reshape(n_q, 1, n_ps), (n_q, answer_len, n_ps))
    live_rows = live_rows.reshape(n_q * answer_len, n_ps).astype(jnp.bfloat16)
    width = -(-(blocks + 2) // 128) * 128
    cols = jnp.arange(width, dtype=jnp.int32)[None, :]
    ps_block = jnp.arange(n_ps, dtype=jnp.int32)[:, None] // tokens
    block_of = ((ps_block == cols) | (cols == blocks)).astype(jnp.bfloat16)
    o_h, aux = _attention(q_h, k_h, v_h, live_rows, block_of)
    aux = aux.reshape(heads, n_q, answer_len, width)
    e_pass = aux[..., :blocks]
    l_loc = aux[..., blocks]
    m_loc = aux[..., width - 1]
    sel = onehot.astype(jnp.bfloat16)
    e_slot = sum(
        jnp.einsum("hqtp,qpj->hqtj", part, sel, preferred_element_type=jnp.float32)
        for part in _split_terms(e_pass, 2)
    )
    o_loc = o_h.reshape(heads, n_q, answer_len, HS)

    n_local_q = n_q // n_dp
    def split_q(a):
        return a.reshape(a.shape[:1] + (nz, nx, n_local_q) + a.shape[2:])
    state = jax.tree.map(split_q, (m_loc, l_loc, o_loc, e_slot))
    state = _reduce_ring(state, 2, xi, nx, xf, xb)
    if nz & (nz - 1) == 0:
        state = _halving(state, zi, nz, lambda b: [(z * nx + x, (z ^ b) * nx + x) for z in range(nz) for x in range(nx)])
    else:
        state = _reduce_ring(state, 1, zi, nz, zf, zb)
    m_fin, l_fin, o_fin, e_fin = state
    context = jnp.transpose(o_fin / l_fin[..., None], (1, 2, 0, 3))
    context = context.reshape(n_local_q, answer_len, inner).astype(jnp.bfloat16)
    mass = jnp.sum(e_fin / l_fin[..., None], axis=(0, 2)) / answer_len
    mass = lax.psum(mass, ("section", "mp"))
    return (context, mass)


def solution(mesh):
    nz, nx = _plane_shape(mesh)
    in_specs = (
        P("dp", None, None),
        P(),
        P("dp", ("section", "mp")),
        P("dp", ("section", "mp")),
        P("dp"),
        P(),
        P("dp", None, ("section", "mp")),
    )
    out_specs = (P("dp", None, ("section", "mp")), P("dp", None))

    def body(*args):
        return _local(nz, nx, *args)

    return jax.shard_map(body, mesh=mesh, in_specs=in_specs, out_specs=out_specs, check_vma=False)
```
